256 devices in a mesh: rep: 64 (over y, x, z_lo), slab: 4 (over z_hi, core).
Axes of the slice: x: 4, y: 4, z: 8 (z_hi: 2, z_lo: 4; z = z_hi * 4 + z_lo), core: 2. Of those that a mesh axis runs over, the one named last changes fastest.
Arguments:
- positions: float32 [64, 3, 16384], P('rep', None, 'slab'), may hold values from 0 to 2
- velocities: float32 [64, 3, 16384], P('rep', None, 'slab'), may hold values from -6 to 6
- inv_mass: float32 [16384], P('slab'), may hold values from 0.5 to 2
- strength: float32 [16384], P('slab'), may hold values from 0.5 to 2
- charge: float32 [16384], P('slab'), may hold values from -1 to 1
- scaling: float32 [64], P('rep'), may hold values from 0.3 to 1
- tile_pairs: int32 [64, 2, 768], P('rep', None, 'slab'), may hold values from 0 to 79, as said below
- tile_counts: int32 [64, 4], P('rep', 'slab'), may hold values from 24 to 192, as said below
- halo_clusters: int32 [64, 64], P('rep', 'slab'), may hold values from 0 to 63, as said below
- swap_pairs: int32 [16, 2], replicated, may hold values from 0 to 63, as said below
Outputs:
- new_positions: float32 [64, 3, 16384], P('rep', None, 'slab')
- new_velocities: float32 [64, 3, 16384], P('rep', None, 'slab')
- potential: float32 [64], P('rep')
The draws below stay inside these ranges and needn't reach their ends.
Inputs may be any that keep to these rules, and one draw needn't show every extreme that they name: `tile_pairs`: for each replica and slab, the 192 columns are distinct tiles (i, j) with i a cluster of that slab and i <= j; j below 64 is a cluster of the same slab, j = 64 + h is halo slot h. Only the first tile_counts columns are live. `tile_counts`: in every replica some slab has all 192 tiles live. `halo_clusters`: the 16 clusters of each replica and slab are distinct. `swap_pairs`: no replica appears twice. The first pair joins two replicas 64 // 2 apart (counted round), the second two neighbouring replicas (counted round); the others are arbitrary.
All inputs are finite; a program needn't handle non-finite values.
Results may differ from the reference program's by a relative error of at most 0.0003.
Values sent between devices are 32-bit elements; how exact they have to be, the bound alone decides.
No kernel may reach another device: no remote copies, remote signals or barrier semaphores. Data moves between devices by JAX's collectives and lax.ppermute only.
A program may use at most 64 MiB of HBM per device.

```python
import math
import jax
import jax.numpy as jnp
from jax import lax

CL = 64
CD = 64
STEPS = 4
HALO = 16
NT_MAX = 192
REPLICAS = 64
SLABS = 4
ATOMS = 16384
PAIRS = 16


def one_tile_list(device_key):
    total_codes = CD * (CD + HALO)
    codes = jnp.arange(total_codes, dtype=jnp.int32)
    first_idx = codes // (CD + HALO)
    second_idx = codes % (CD + HALO)
    valid = second_idx >= first_idx
    shuffled = jax.random.permutation(device_key, total_codes).astype(jnp.int32)
    scores = jnp.where(valid, shuffled, total_codes + codes)
    chosen = jnp.argsort(scores, stable=True)[:NT_MAX]
    return jnp.stack([first_idx[chosen], second_idx[chosen]], 0).astype(jnp.int32)


def draw_tile_pairs(key, part):
    device_keys = jax.random.split(jax.random.fold_in(key, 11), REPLICAS * SLABS)
    listed = jax.vmap(one_tile_list)(device_keys)
    listed = listed.reshape(REPLICAS, SLABS, 2, NT_MAX).transpose(0, 2, 1, 3)
    return listed.reshape(REPLICAS, 2, SLABS * NT_MAX).astype(jnp.int32)


def draw_tile_counts(key, part):
    key_full, key_rest = jax.random.split(jax.random.fold_in(key, 23))
    full_slab = jax.random.randint(key_full, (REPLICAS,), 0, SLABS)
    others = jax.random.randint(key_rest, (REPLICAS, SLABS), NT_MAX // 8, NT_MAX // 2 + 1)
    slab_ids = jnp.arange(SLABS, dtype=jnp.int32)
    return jnp.where(slab_ids[None, :] == full_slab[:, None], NT_MAX, others).astype(jnp.int32)


def one_halo_list(device_key):
    return jax.random.permutation(device_key, CD)[:HALO].astype(jnp.int32)


def draw_halo_clusters(key, part):
    device_keys = jax.random.split(jax.random.fold_in(key, 37), REPLICAS * SLABS)
    listed = jax.vmap(one_halo_list)(device_keys)
    return listed.reshape(REPLICAS, SLABS * HALO).astype(jnp.int32)


def draw_swap_pairs(key, part):
    key_anchor, key_rest = jax.random.split(jax.random.fold_in(key, 53))
    anchor = jax.random.randint(key_anchor, (), 0, REPLICAS).astype(jnp.int32)
    opposite = ((anchor + REPLICAS // 2) % REPLICAS).astype(jnp.int32)
    near_low = ((anchor + 1) % REPLICAS).astype(jnp.int32)
    near_high = ((anchor + 2) % REPLICAS).astype(jnp.int32)
    shuffled = jax.random.permutation(key_rest, REPLICAS).astype(jnp.int32)
    ranks = jnp.zeros((REPLICAS,), jnp.int32).at[shuffled].set(jnp.arange(REPLICAS, dtype=jnp.int32))
    replica_ids = jnp.arange(REPLICAS, dtype=jnp.int32)
    taken = (replica_ids == anchor) | (replica_ids == opposite) | (replica_ids == near_low) | (replica_ids == near_high)
    scores = jnp.where(taken, REPLICAS + replica_ids, ranks)
    order = jnp.argsort(scores, stable=True).astype(jnp.int32)
    rest = order[:2 * PAIRS - 4]
    fixed_pairs = jnp.stack([anchor, opposite, near_low, near_high])
    return jnp.concatenate([fixed_pairs, rest], 0).reshape(PAIRS, 2).astype(jnp.int32)


def steps_of(key, dims, shards, low, top_value):
    def one(dim, blocks):
        steps = jax.random.uniform(jax.random.fold_in(jax.random.fold_in(key, 6), dim), (blocks,), jnp.float32, low / len(shards), top_value / len(shards))
        return jnp.repeat(jnp.exp(steps), dims[dim] // blocks).reshape((-1,) + (1,) * (len(dims) - dim - 1))

    gain = one(*shards[0])
    for cut in shards[1:]:
        gain = gain * one(*cut)
    return gain


def gaussian(own_key, extent, spread, limit, shards=(), held_as=jnp.bfloat16):
    values = jax.random.normal(own_key, extent, jnp.float32) * spread
    if len(shards) > 0:
        values = steps_of(own_key, extent, shards, -0.22, 0.18) * values
    return jnp.clip(values, min=-limit, max=limit).astype(held_as)


def setup_inputs(seed: int = 0) -> dict:
    key_list = jax.random.split(jax.random.key(seed), 11)
    positions = jnp.clip(2.0 * jax.random.uniform(key_list[0], (REPLICAS, 3, ATOMS), jnp.float32) ** steps_of(key_list[0], (REPLICAS, 3, ATOMS), ((0, 64), (2, 4)), -0.2, 0.2), 0.0, 2.0)
    velocities = gaussian(key_list[1], (REPLICAS, 3, ATOMS), 1.0, 6.0, ((0, 64), (2, 4)), jnp.float32)
    inv_mass = jnp.clip(jnp.exp(math.log(2.0) - 1.3862944 * jax.random.uniform(key_list[2], (ATOMS,), jnp.float32) ** steps_of(key_list[2], (ATOMS,), ((0, 4),), -0.2, 0.2)), 0.5, 2.0)
    strength = jnp.clip(jnp.exp(math.log(2.0) - 1.3862944 * jax.random.uniform(key_list[3], (ATOMS,), jnp.float32) ** steps_of(key_list[3], (ATOMS,), ((0, 4),), -0.2, 0.2)), 0.5, 2.0)
    charge = jnp.clip(jax.random.uniform(key_list[4], (ATOMS,), jnp.float32, -1.0, 1.0) * steps_of(key_list[4], (ATOMS,), ((0, 4),), -0.4, 0.0), -1.0, 1.0)
    scaling = jnp.clip(jnp.exp(math.log(1.0) - 1.2039728 * jax.random.uniform(key_list[5], (REPLICAS,), jnp.float32) ** steps_of(key_list[5], (REPLICAS,), ((0, 64),), -0.2, 0.2)), 0.3, 1.0)
    tile_pairs = draw_tile_pairs(jax.random.fold_in(key_list[10], 71), 0)
    tile_counts = draw_tile_counts(jax.random.fold_in(key_list[10], 71), 0)
    halo_clusters = draw_halo_clusters(jax.random.fold_in(key_list[10], 71), 0)
    swap_pairs = draw_swap_pairs(jax.random.fold_in(key_list[10], 71), 0)
    return {"positions": positions, "velocities": velocities, "inv_mass": inv_mass, "strength": strength, "charge": charge, "scaling": scaling, "tile_pairs": tile_pairs, "tile_counts": tile_counts, "halo_clusters": halo_clusters, "swap_pairs": swap_pairs}


tile_block = 16
time_step = 0.04
half_step = 0.02
soft_sq = 0.25
slab_width = 2.0

def partner_of(pair_list, replica_ids):
    first_col = pair_list[:, 0]
    second_col = pair_list[:, 1]
    hit_first = replica_ids[:, None] == first_col[None, :]
    hit_second = replica_ids[:, None] == second_col[None, :]
    partner_sum = lax.optimization_barrier(jnp.sum(jnp.where(hit_first, second_col[None, :], 0), 1)) + lax.optimization_barrier(jnp.sum(jnp.where(hit_second, first_col[None, :], 0), 1))
    listed = jnp.any(hit_first, 1) | jnp.any(hit_second, 1)
    return jnp.where(listed, partner_sum, replica_ids).astype(jnp.int32)

def pair_block(extended, strength_all, charge_all, ham_scale, tile_first, tile_second, live_mask):
    count_tiles = tile_first.shape[0]
    coords_i = jnp.take(extended, tile_first, axis=1).transpose(0, 2, 1)
    coords_j = jnp.take(extended, tile_second, axis=1)
    offsets = (coords_i[:, :, :, None] - coords_j[:, None, :, :]).reshape(3, CL, count_tiles * CL)
    sq_dist = offsets[0] * offsets[0] + offsets[1] * offsets[1] + offsets[2] * offsets[2]
    strength_i = jnp.take(strength_all, tile_first, axis=0).T
    strength_j = jnp.take(strength_all, tile_second, axis=0)
    charge_i = jnp.take(charge_all, tile_first, axis=0).T
    charge_j = jnp.take(charge_all, tile_second, axis=0)
    strength_prod = (strength_i[:, :, None] * strength_j[None, :, :]).reshape(CL, count_tiles * CL)
    charge_prod = (charge_i[:, :, None] * charge_j[None, :, :]).reshape(CL, count_tiles * CL)
    gauss_term = strength_prod * jnp.exp(-sq_dist)
    inv_root = lax.rsqrt(sq_dist + soft_sq)
    coulomb = ham_scale * charge_prod * inv_root
    same_tile = tile_first == tile_second
    weight_tile = jnp.where(live_mask, jnp.where(same_tile, 0.5, 1.0), 0.0).astype(jnp.float32)
    weight_col = jnp.repeat(weight_tile, CL)[None, :]
    slope = gauss_term + 0.5 * coulomb * inv_root * inv_root
    pushes = (2.0 * slope * weight_col)[None, :, :] * offsets
    force_i = pushes.reshape(3, CL, count_tiles, CL).sum(-1).transpose(0, 2, 1)
    force_j = -pushes.sum(1).reshape(3, count_tiles, CL)
    atom_ids = jnp.arange(CL, dtype=jnp.int32)
    column_ids = jnp.arange(count_tiles * CL, dtype=jnp.int32) % CL
    self_pair = jnp.repeat(same_tile, CL)[None, :] & (atom_ids[:, None] == column_ids[None, :])
    energy = jnp.sum(jnp.where(self_pair, 0.0, (gauss_term + coulomb) * weight_col))
    return (force_i, force_j, energy)

def slab_forces(extended, strength_all, charge_all, ham_scale, tile_list, live_count):
    firsts = tile_list[0].reshape(-1, tile_block)
    seconds = tile_list[1].reshape(-1, tile_block)
    slot_ids = jnp.arange(NT_MAX, dtype=jnp.int32).reshape(-1, tile_block)

    def visit_block(totals, inputs):
        tile_first, tile_second, slot_row = inputs
        force_i, force_j, energy_part = pair_block(extended, strength_all, charge_all, ham_scale, tile_first, tile_second, slot_row < live_count)
        forces = totals[0].at[:, tile_first].add(force_i).at[:, tile_second].add(force_j)
        return ((forces, totals[1] + energy_part), None)
    start_state = (jnp.zeros((3, CD + HALO, CL), jnp.float32), jnp.zeros((), jnp.float32))
    result, _ = lax.scan(visit_block, start_state, (firsts, seconds, slot_ids))
    return result

def reference(positions, velocities, inv_mass, strength, charge, scaling, tile_pairs, tile_counts, halo_clusters, swap_pairs):
    strength_blocks = strength.reshape(SLABS, CD, CL)
    charge_blocks = charge.reshape(SLABS, CD, CL)
    lift = jnp.array([0.0, 0.0, slab_width], jnp.float32)[:, None, None]

    def one_replica(inputs):
        coords, speeds, ham_scale, tile_list, live_counts, halo_list = inputs

        def evaluate(coords_now):
            blocks = coords_now.reshape(3, SLABS, CD, CL)
            totals = jnp.zeros((3, SLABS, CD, CL), jnp.float32)
            energy = jnp.zeros((), jnp.float32)
            for slab_idx in range(SLABS):
                upper_slab = (slab_idx + 1) % SLABS
                sent_ids = halo_list[upper_slab * HALO:(upper_slab + 1) * HALO]
                from_above = jnp.take(blocks[:, upper_slab], sent_ids, axis=1) + lift
                extended = jnp.concatenate([blocks[:, slab_idx], from_above], 1)
                strength_all = jnp.concatenate([strength_blocks[slab_idx], jnp.take(strength_blocks[upper_slab], sent_ids, axis=0)], 0)
                charge_all = jnp.concatenate([charge_blocks[slab_idx], jnp.take(charge_blocks[upper_slab], sent_ids, axis=0)], 0)
                forces, energy_part = slab_forces(extended, strength_all, charge_all, ham_scale, tile_list[:, slab_idx * NT_MAX:(slab_idx + 1) * NT_MAX], live_counts[slab_idx])
                totals = totals.at[:, slab_idx].add(forces[:, :CD])
                totals = totals.at[:, upper_slab, sent_ids].add(forces[:, CD:])
                energy = energy + energy_part
            return (totals.reshape(3, ATOMS), energy)
        forces, energy = evaluate(coords)
        for step_idx in range(STEPS):
            speeds = speeds + half_step * forces * inv_mass
            coords = coords + time_step * speeds
            forces, energy = evaluate(coords)
            speeds = speeds + half_step * forces * inv_mass
        return (coords, speeds, energy)
    moved_pos, moved_vel, energies = lax.map(one_replica, (positions, velocities, scaling, tile_pairs, tile_counts, halo_clusters))
    partner = partner_of(swap_pairs, jnp.arange(REPLICAS, dtype=jnp.int32))
    new_positions = jnp.take(moved_pos, partner, axis=0)
    new_velocities = jnp.take(moved_vel, partner, axis=0)
    return (new_positions, new_velocities, energies / ATOMS)
```

```python
import jax
import jax.numpy as jnp
from jax import lax
from jax.sharding import PartitionSpec as P

CL = 64
CD = 64
STEPS = 4
HALO = 16
NT_MAX = 192


tile_block = 16
time_step = 0.04
half_step = 0.02
soft_sq = 0.25
slab_width = 2.0
exact = lax.Precision.HIGHEST


def from_behind(value, axis, steps):
    count = lax.axis_size(axis)
    pairs = [(source, (source + steps) % count) for source in range(count)]
    return lax.ppermute(value, axis, pairs)


def partner_of(pair_list, replica_ids):
    first_col = pair_list[:, 0]
    second_col = pair_list[:, 1]
    hit_first = replica_ids[:, None] == first_col[None, :]
    hit_second = replica_ids[:, None] == second_col[None, :]
    partner_sum = jnp.sum(jnp.where(hit_first, second_col[None, :], 0), 1) + jnp.sum(
        jnp.where(hit_second, first_col[None, :], 0), 1
    )
    listed = jnp.any(hit_first, 1) | jnp.any(hit_second, 1)
    return jnp.where(listed, partner_sum, replica_ids)


def exchange(state, swap_pairs):
    count = lax.axis_size("rep")
    rows, width = state.shape
    partner = partner_of(swap_pairs, jnp.arange(count, dtype=jnp.int32))
    chunks = state.reshape(rows, count, width // count).transpose(1, 0, 2)
    spread = lax.all_to_all(chunks, "rep", 0, 0, tiled=True)
    routed = jnp.take(spread, partner, axis=0)
    gathered = lax.all_to_all(routed, "rep", 0, 0, tiled=True)
    return gathered.transpose(1, 0, 2).reshape(rows, width)


def select_table(index_list, width):
    cluster_ids = jnp.arange(width, dtype=jnp.int32)
    return (index_list[:, None] == cluster_ids[None, :]).astype(jnp.float32)


def pair_block(extended, strength_all, charge_all, ham_scale, tile_first, tile_second, live_mask):
    count_tiles = tile_first.shape[0]
    width = extended.shape[1]
    select_first = select_table(tile_first, width)
    select_second = select_table(tile_second, width)
    coords_i = jnp.einsum("te,xec->xct", select_first, extended, precision=exact)
    coords_j = jnp.einsum("te,xec->xtc", select_second, extended, precision=exact)
    offsets = (coords_i[:, :, :, None] - coords_j[:, None, :, :]).reshape(3, CL, count_tiles * CL)
    sq_dist = offsets[0] * offsets[0] + offsets[1] * offsets[1] + offsets[2] * offsets[2]
    params_all = jnp.stack([strength_all, charge_all], 0)
    params_i = jnp.einsum("te,pec->pct", select_first, params_all, precision=exact)
    params_j = jnp.einsum("te,pec->ptc", select_second, params_all, precision=exact)
    strength_prod = (params_i[0][:, :, None] * params_j[0][None, :, :]).reshape(
        CL, count_tiles * CL
    )
    charge_prod = (params_i[1][:, :, None] * params_j[1][None, :, :]).reshape(CL, count_tiles * CL)
    gauss_term = strength_prod * jnp.exp(-sq_dist)
    inv_root = lax.rsqrt(sq_dist + soft_sq)
    coulomb = ham_scale * charge_prod * inv_root
    same_tile = tile_first == tile_second
    weight_tile = jnp.where(live_mask, jnp.where(same_tile, 0.5, 1.0), 0.0).astype(jnp.float32)
    weight_col = jnp.repeat(weight_tile, CL)[None, :]
    slope = gauss_term + 0.5 * coulomb * inv_root * inv_root
    pushes = (2.0 * slope * weight_col)[None, :, :] * offsets
    force_i = pushes.reshape(3, CL, count_tiles, CL).sum(-1)
    force_j = -pushes.sum(1).reshape(3, count_tiles, CL)
    atom_ids = jnp.arange(CL, dtype=jnp.int32)
    column_ids = jnp.arange(count_tiles * CL, dtype=jnp.int32) % CL
    self_pair = jnp.repeat(same_tile, CL)[None, :] & (atom_ids[:, None] == column_ids[None, :])
    energy = jnp.sum(jnp.where(self_pair, 0.0, (gauss_term + coulomb) * weight_col))
    spread_i = jnp.einsum("te,xct->xec", select_first, force_i, precision=exact)
    spread_j = jnp.einsum("te,xtc->xec", select_second, force_j, precision=exact)
    return (spread_i + spread_j, energy)


def local(
    positions,
    velocities,
    inv_mass,
    strength,
    charge,
    scaling,
    tile_pairs,
    tile_counts,
    halo_clusters,
    swap_pairs,
):
    coords = positions[0]
    speeds = velocities[0]
    ham_scale = scaling[0]
    firsts_flat = tile_pairs[0, 0]
    seconds_flat = tile_pairs[0, 1]
    live_count = tile_counts[0, 0]
    halo_index = halo_clusters[0]
    atoms_here = coords.shape[1]
    halo_table = select_table(halo_index, CD)
    params = jnp.stack([strength, charge], 0).reshape(2, CD, CL)
    sent_params = jnp.einsum("hc,pck->phk", halo_table, params, precision=exact).reshape(
        2, HALO * CL
    )
    got_params = from_behind(sent_params, "slab", -1).reshape(2, HALO, CL)
    strength_all = jnp.concatenate([params[0], got_params[0]], 0)
    charge_all = jnp.concatenate([params[1], got_params[1]], 0)
    lift = jnp.array([0.0, 0.0, slab_width], jnp.float32)[:, None]
    extended_now = [None]

    def add_block(totals, tile_first, tile_second, slot_row):
        spread, energy_part = pair_block(
            extended_now[0],
            strength_all,
            charge_all,
            ham_scale,
            tile_first,
            tile_second,
            slot_row < live_count,
        )
        return (totals[0] + spread, totals[1] + energy_part)

    def evaluate(coords_now):
        blocks = coords_now.reshape(3, CD, CL)
        sent_coords = jnp.einsum("hc,xck->xhk", halo_table, blocks, precision=exact).reshape(
            3, HALO * CL
        )
        from_above = from_behind(sent_coords, "slab", -1) + lift
        extended_now[0] = jnp.concatenate([blocks, from_above.reshape(3, HALO, CL)], 1)
        start_state = (jnp.zeros((3, CD + HALO, CL), jnp.float32), jnp.zeros((), jnp.float32))
        firsts = firsts_flat.reshape(-1, tile_block)
        seconds = seconds_flat.reshape(-1, tile_block)
        slot_ids = jnp.arange(NT_MAX, dtype=jnp.int32).reshape(-1, tile_block)

        def visit_block(totals, inputs):
            return (add_block(totals, inputs[0], inputs[1], inputs[2]), None)

        result, _ = lax.scan(visit_block, start_state, (firsts, seconds, slot_ids))
        forces, energy = result
        returned = from_behind(forces[:, CD:].reshape(3, HALO * CL), "slab", 1)
        back_home = jnp.einsum(
            "hc,xhk->xck", halo_table, returned.reshape(3, HALO, CL), precision=exact
        )
        local_forces = forces[:, :CD] + back_home
        return (local_forces.reshape(3, atoms_here), energy)

    forces, energy = evaluate(coords)
    for step_idx in range(STEPS):
        speeds = speeds + half_step * forces * inv_mass
        coords = coords + time_step * speeds
        forces, energy = evaluate(coords)
        speeds = speeds + half_step * forces * inv_mass
    total_energy = lax.psum(energy, "slab")
    potential = (total_energy / (atoms_here * lax.axis_size("slab"))).reshape(1)
    state = jnp.concatenate([coords, speeds], 0)
    swapped = exchange(state, swap_pairs)
    return (swapped[:3][None], swapped[3:][None], potential)


def solution(mesh):
    in_specs = (
        P("rep", None, "slab"),
        P("rep", None, "slab"),
        P("slab"),
        P("slab"),
        P("slab"),
        P("rep"),
        P("rep", None, "slab"),
        P("rep", "slab"),
        P("rep", "slab"),
        P(),
    )
    out_specs = (P("rep", None, "slab"), P("rep", None, "slab"), P("rep"))
    return jax.shard_map(local, mesh=mesh, in_specs=in_specs, out_specs=out_specs, check_vma=False)
```

```python
import jax
import jax.numpy as jnp
from jax import lax
from jax.sharding import PartitionSpec as P
from jax.experimental import pallas as pl
from jax.experimental.pallas import tpu as pltpu

CL = 64
CD = 64
STEPS = 4
HALO = 16
NT_MAX = 192
HALF = CL // 2


tile_block = 16
time_step = 0.04
half_step = 0.02
soft_sq = 0.25
slab_width = 2.0
exact = lax.Precision.HIGHEST


def pair_kernel(tiles_ref, count_ref, xcol_ref, xrow_ref, pcol_ref, prow_ref, wsame_ref,
                fcol_ref, frow_ref, en_ref):
    fcol_ref[...] = jnp.zeros(fcol_ref.shape, jnp.float32)
    frow_ref[...] = jnp.zeros(frow_ref.shape, jnp.float32)

    def body(t, acc):
        i = tiles_ref[0, t]
        j = tiles_ref[1, t]
        dx = xcol_ref[0, i] - xrow_ref[0, j]
        dy = xcol_ref[1, i] - xrow_ref[1, j]
        dz = xcol_ref[2, i] - xrow_ref[2, j]
        sq = dx * dx + dy * dy + dz * dz
        gauss = pcol_ref[0, i] * prow_ref[0, j] * jnp.exp(-sq)
        inv_root = lax.rsqrt(sq + soft_sq)
        coulomb = pcol_ref[1, i] * prow_ref[1, j] * inv_root
        same = i == j
        w_force = jnp.where(same, 0.5, 1.0).astype(jnp.float32)
        w_energy = jnp.where(same, wsame_ref[...], 1.0)
        slope = w_force * (2.0 * gauss + coulomb * inv_root * inv_root)
        px = slope * dx
        py = slope * dy
        pz = slope * dz
        fcol_ref[0, i] += px
        fcol_ref[1, i] += py
        fcol_ref[2, i] += pz
        frow_ref[0, j] -= jnp.sum(px, axis=0, keepdims=True)
        frow_ref[1, j] -= jnp.sum(py, axis=0, keepdims=True)
        frow_ref[2, j] -= jnp.sum(pz, axis=0, keepdims=True)
        return acc + w_energy * (gauss + coulomb)

    acc = lax.fori_loop(0, count_ref[0], body, jnp.zeros((HALF, 2 * CL), jnp.float32))
    en_ref[...] = acc


def self_weights():
    rows = lax.broadcasted_iota(jnp.int32, (HALF, 2 * CL), 0)
    lanes = lax.broadcasted_iota(jnp.int32, (HALF, 2 * CL), 1)
    return jnp.where(2 * rows + lanes // CL == lanes % CL, 0.0, 0.5).astype(jnp.float32)


def as_columns(values):
    lead = values.shape[:-1]
    return jnp.repeat(values.reshape(lead + (HALF, 2)), CL, axis=-1)


def as_rows(values):
    lead = values.shape[:-1]
    return jnp.concatenate([values, values], -1).reshape(lead + (1, 2 * CL))


def slab_pairs(extended, pcol, prow, tiles, count):
    width = extended.shape[1]
    xcol = as_columns(extended)
    xrow = as_rows(extended)
    smem = pl.BlockSpec(memory_space=pltpu.SMEM)
    vmem = pl.BlockSpec(memory_space=pltpu.VMEM)
    fcol, frow, acc = pl.pallas_call(
        pair_kernel,
        out_shape=(
            jax.ShapeDtypeStruct((3, width, HALF, 2 * CL), jnp.float32),
            jax.ShapeDtypeStruct((3, width, 1, 2 * CL), jnp.float32),
            jax.ShapeDtypeStruct((HALF, 2 * CL), jnp.float32),
        ),
        in_specs=[smem, smem, vmem, vmem, vmem, vmem, vmem],
        out_specs=(vmem, vmem, vmem),
        compiler_params=pltpu.CompilerParams(vmem_limit_bytes=48 * 1024 * 1024),
    )(tiles, count.reshape(1), xcol, xrow, pcol, prow, self_weights())
    f_i = fcol.reshape(3, width, HALF, 2, CL).sum(-1).reshape(3, width, CL)
    f_j = frow.reshape(3, width, 2, CL).sum(2)
    return f_i + f_j, jnp.sum(acc)


def from_behind(value, axis, steps):
    count = lax.axis_size(axis)
    pairs = [(source, (source + steps) % count) for source in range(count)]
    return lax.ppermute(value, axis, pairs)


def partner_of(pair_list, replica_ids):
    first_col = pair_list[:, 0]
    second_col = pair_list[:, 1]
    hit_first = replica_ids[:, None] == first_col[None, :]
    hit_second = replica_ids[:, None] == second_col[None, :]
    partner_sum = jnp.sum(jnp.where(hit_first, second_col[None, :], 0), 1) + jnp.sum(
        jnp.where(hit_second, first_col[None, :], 0), 1
    )
    listed = jnp.any(hit_first, 1) | jnp.any(hit_second, 1)
    return jnp.where(listed, partner_sum, replica_ids)


def exchange(state, swap_pairs):
    count = lax.axis_size("rep")
    rows, width = state.shape
    partner = partner_of(swap_pairs, jnp.arange(count, dtype=jnp.int32))
    chunks = state.reshape(rows, count, width // count).transpose(1, 0, 2)
    spread = lax.all_to_all(chunks, "rep", 0, 0, tiled=True)
    routed = jnp.take(spread, partner, axis=0)
    gathered = lax.all_to_all(routed, "rep", 0, 0, tiled=True)
    return gathered.transpose(1, 0, 2).reshape(rows, width)


def select_table(index_list, width):
    cluster_ids = jnp.arange(width, dtype=jnp.int32)
    return (index_list[:, None] == cluster_ids[None, :]).astype(jnp.float32)


def pair_block(extended, strength_all, charge_all, ham_scale, tile_first, tile_second, live_mask):
    count_tiles = tile_first.shape[0]
    width = extended.shape[1]
    select_first = select_table(tile_first, width)
    select_second = select_table(tile_second, width)
    coords_i = jnp.einsum("te,xec->xct", select_first, extended, precision=exact)
    coords_j = jnp.einsum("te,xec->xtc", select_second, extended, precision=exact)
    offsets = (coords_i[:, :, :, None] - coords_j[:, None, :, :]).reshape(3, CL, count_tiles * CL)
    sq_dist = offsets[0] * offsets[0] + offsets[1] * offsets[1] + offsets[2] * offsets[2]
    params_all = jnp.stack([strength_all, charge_all], 0)
    params_i = jnp.einsum("te,pec->pct", select_first, params_all, precision=exact)
    params_j = jnp.einsum("te,pec->ptc", select_second, params_all, precision=exact)
    strength_prod = (params_i[0][:, :, None] * params_j[0][None, :, :]).reshape(
        CL, count_tiles * CL
    )
    charge_prod = (params_i[1][:, :, None] * params_j[1][None, :, :]).reshape(CL, count_tiles * CL)
    gauss_term = strength_prod * jnp.exp(-sq_dist)
    inv_root = lax.rsqrt(sq_dist + soft_sq)
    coulomb = ham_scale * charge_prod * inv_root
    same_tile = tile_first == tile_second
    weight_tile = jnp.where(live_mask, jnp.where(same_tile, 0.5, 1.0), 0.0).astype(jnp.float32)
    weight_col = jnp.repeat(weight_tile, CL)[None, :]
    slope = gauss_term + 0.5 * coulomb * inv_root * inv_root
    pushes = (2.0 * slope * weight_col)[None, :, :] * offsets
    force_i = pushes.reshape(3, CL, count_tiles, CL).sum(-1)
    force_j = -pushes.sum(1).reshape(3, count_tiles, CL)
    atom_ids = jnp.arange(CL, dtype=jnp.int32)
    column_ids = jnp.arange(count_tiles * CL, dtype=jnp.int32) % CL
    self_pair = jnp.repeat(same_tile, CL)[None, :] & (atom_ids[:, None] == column_ids[None, :])
    energy = jnp.sum(jnp.where(self_pair, 0.0, (gauss_term + coulomb) * weight_col))
    spread_i = jnp.einsum("te,xct->xec", select_first, force_i, precision=exact)
    spread_j = jnp.einsum("te,xtc->xec", select_second, force_j, precision=exact)
    return (spread_i + spread_j, energy)


def local(
    positions,
    velocities,
    inv_mass,
    strength,
    charge,
    scaling,
    tile_pairs,
    tile_counts,
    halo_clusters,
    swap_pairs,
):
    coords = positions[0]
    speeds = velocities[0]
    ham_scale = scaling[0]
    firsts_flat = tile_pairs[0, 0]
    seconds_flat = tile_pairs[0, 1]
    live_count = tile_counts[0, 0]
    halo_index = halo_clusters[0]
    atoms_here = coords.shape[1]
    halo_table = select_table(halo_index, CD)
    params = jnp.stack([strength, charge], 0).reshape(2, CD, CL)
    sent_params = jnp.einsum("hc,pck->phk", halo_table, params, precision=exact).reshape(
        2, HALO * CL
    )
    got_params = from_behind(sent_params, "slab", -1).reshape(2, HALO, CL)
    strength_all = jnp.concatenate([params[0], got_params[0]], 0)
    charge_all = jnp.concatenate([params[1], got_params[1]], 0)
    lift = jnp.array([0.0, 0.0, slab_width], jnp.float32)[:, None]
    param_cols = jnp.stack([as_columns(strength_all), as_columns(ham_scale * charge_all)], 0)
    param_rows = jnp.stack([as_rows(strength_all), as_rows(charge_all)], 0)
    tile_list = jnp.stack([firsts_flat, seconds_flat], 0)

    def evaluate(coords_now):
        blocks = coords_now.reshape(3, CD, CL)
        sent_coords = jnp.einsum("hc,xck->xhk", halo_table, blocks, precision=exact).reshape(
            3, HALO * CL
        )
        from_above = from_behind(sent_coords, "slab", -1) + lift
        extended = jnp.concatenate([blocks, from_above.reshape(3, HALO, CL)], 1)
        forces, energy = slab_pairs(extended, param_cols, param_rows, tile_list, live_count)
        returned = from_behind(forces[:, CD:].reshape(3, HALO * CL), "slab", 1)
        back_home = jnp.einsum(
            "hc,xhk->xck", halo_table, returned.reshape(3, HALO, CL), precision=exact
        )
        local_forces = forces[:, :CD] + back_home
        return (local_forces.reshape(3, atoms_here), energy)

    def verlet_step(step_idx, carry):
        coords, speeds, forces, energy = carry
        speeds = speeds + half_step * forces * inv_mass
        coords = coords + time_step * speeds
        forces, energy = evaluate(coords)
        speeds = speeds + half_step * forces * inv_mass
        return (coords, speeds, forces, energy)

    forces, energy = evaluate(coords)
    coords, speeds, forces, energy = lax.fori_loop(
        0, STEPS, verlet_step, (coords, speeds, forces, energy)
    )
    total_energy = lax.psum(energy, "slab")
    potential = (total_energy / (atoms_here * lax.axis_size("slab"))).reshape(1)
    state = jnp.concatenate([coords, speeds], 0)
    swapped = exchange(state, swap_pairs)
    return (swapped[:3][None], swapped[3:][None], potential)


def solution(mesh):
    in_specs = (
        P("rep", None, "slab"),
        P("rep", None, "slab"),
        P("slab"),
        P("slab"),
        P("slab"),
        P("rep"),
        P("rep", None, "slab"),
        P("rep", "slab"),
        P("rep", "slab"),
        P(),
    )
    out_specs = (P("rep", None, "slab"), P("rep", None, "slab"), P("rep"))
    return jax.shard_map(local, mesh=mesh, in_specs=in_specs, out_specs=out_specs, check_vma=False)
```

```python
import jax
import jax.numpy as jnp
from jax import lax
from jax.sharding import PartitionSpec as P
from jax.experimental import pallas as pl
from jax.experimental.pallas import tpu as pltpu

CL = 64
CD = 64
STEPS = 4
HALO = 16
NT_MAX = 192
HALF = CL // 2


tile_block = 16
time_step = 0.04
half_step = 0.02
soft_sq = 0.25
slab_width = 2.0
exact = lax.Precision.HIGHEST


def spread_masks():
    rows = lax.broadcasted_iota(jnp.int32, (HALF, CL), 0)
    atoms = lax.broadcasted_iota(jnp.int32, (HALF, CL), 1)
    pick = (atoms // 2 == rows).astype(jnp.float32)
    atoms_t = lax.broadcasted_iota(jnp.int32, (CL, 2 * CL), 0)
    lanes_t = lax.broadcasted_iota(jnp.int32, (CL, 2 * CL), 1)
    place = (atoms_t % 2 == lanes_t // CL).astype(jnp.float32)
    return pick, place


def to_columns(values, pick, place):
    width = values.shape[0]
    picked = (values[:, None, :] * pick[None]).reshape(width * HALF, CL)
    place_b = place.astype(jnp.bfloat16)
    hi = picked.astype(jnp.bfloat16)
    rest = picked - hi.astype(jnp.float32)
    mid = rest.astype(jnp.bfloat16)
    lo = (rest - mid.astype(jnp.float32)).astype(jnp.bfloat16)
    spread = jnp.dot(hi, place_b, preferred_element_type=jnp.float32)
    spread = spread + jnp.dot(mid, place_b, preferred_element_type=jnp.float32)
    spread = spread + jnp.dot(lo, place_b, preferred_element_type=jnp.float32)
    return spread.reshape(width, HALF, 2 * CL)


def from_columns(blocks, pick, place):
    width = blocks.shape[0]
    folded = lax.dot_general(
        blocks.reshape(width * HALF, 2 * CL), place, (((1,), (1,)), ((), ())),
        precision=exact, preferred_element_type=jnp.float32,
    )
    return jnp.sum(folded.reshape(width, HALF, CL) * pick[None], axis=1)


def pair_kernel(tiles_ref, count_ref, ext_ref, prm_ref, xrow_ref, prow_ref,
                fi_ref, frow_ref, en_ref, xcol_ref, pcol_ref, fcol_ref):
    pick, place = spread_masks()
    for c in range(3):
        xcol_ref[c] = to_columns(ext_ref[c], pick, place)
    for c in range(2):
        pcol_ref[c] = to_columns(prm_ref[c], pick, place)
    fcol_ref[...] = jnp.zeros(fcol_ref.shape, jnp.float32)
    frow_ref[...] = jnp.zeros(frow_ref.shape, jnp.float32)
    rows = lax.broadcasted_iota(jnp.int32, (HALF, 2 * CL), 0)
    lanes = lax.broadcasted_iota(jnp.int32, (HALF, 2 * CL), 1)
    w_same = jnp.where(2 * rows + lanes // CL == lanes % CL, 0.0, 0.5).astype(jnp.float32)

    def body(t, acc):
        i = tiles_ref[0, t]
        j = tiles_ref[1, t]
        dx = xcol_ref[0, i] - xrow_ref[0, j]
        dy = xcol_ref[1, i] - xrow_ref[1, j]
        dz = xcol_ref[2, i] - xrow_ref[2, j]
        sq = dx * dx + dy * dy + dz * dz
        gauss = pcol_ref[0, i] * prow_ref[0, j] * jnp.exp(-sq)
        inv_root = lax.rsqrt(sq + soft_sq)
        coulomb = pcol_ref[1, i] * prow_ref[1, j] * inv_root
        same = i == j
        w_force = jnp.where(same, 0.5, 1.0).astype(jnp.float32)
        w_energy = jnp.where(same, w_same, 1.0)
        slope = w_force * (2.0 * gauss + coulomb * inv_root * inv_root)
        px = slope * dx
        py = slope * dy
        pz = slope * dz
        fcol_ref[0, i] += px
        fcol_ref[1, i] += py
        fcol_ref[2, i] += pz
        frow_ref[0, j] -= jnp.sum(px, axis=0, keepdims=True)
        frow_ref[1, j] -= jnp.sum(py, axis=0, keepdims=True)
        frow_ref[2, j] -= jnp.sum(pz, axis=0, keepdims=True)
        return acc + w_energy * (gauss + coulomb)

    acc = lax.fori_loop(0, count_ref[0], body, jnp.zeros((HALF, 2 * CL), jnp.float32))
    en_ref[...] = acc
    for c in range(3):
        fi_ref[c] = from_columns(fcol_ref[c], pick, place)


def as_rows(values):
    lead = values.shape[:-1]
    return jnp.concatenate([values, values], -1).reshape(lead + (1, 2 * CL))


def slab_pairs(extended, prm_cols, prow, tiles, count):
    width = extended.shape[1]
    xrow = as_rows(extended)
    smem = pl.BlockSpec(memory_space=pltpu.SMEM)
    vmem = pl.BlockSpec(memory_space=pltpu.VMEM)
    f_i, frow, acc = pl.pallas_call(
        pair_kernel,
        out_shape=(
            jax.ShapeDtypeStruct((3, width, CL), jnp.float32),
            jax.ShapeDtypeStruct((3, width, 1, 2 * CL), jnp.float32),
            jax.ShapeDtypeStruct((HALF, 2 * CL), jnp.float32),
        ),
        in_specs=[smem, smem, vmem, vmem, vmem, vmem],
        out_specs=(vmem, vmem, vmem),
        scratch_shapes=[
            pltpu.VMEM((3, width, HALF, 2 * CL), jnp.float32),
            pltpu.VMEM((2, width, HALF, 2 * CL), jnp.float32),
            pltpu.VMEM((3, width, HALF, 2 * CL), jnp.float32),
        ],
        compiler_params=pltpu.CompilerParams(vmem_limit_bytes=48 * 1024 * 1024),
    )(tiles, count.reshape(1), extended, prm_cols, xrow, prow)
    f_j = frow.reshape(3, width, 2, CL).sum(2)
    return f_i + f_j, jnp.sum(acc)


def from_behind(value, axis, steps):
    count = lax.axis_size(axis)
    pairs = [(source, (source + steps) % count) for source in range(count)]
    return lax.ppermute(value, axis, pairs)


def partner_of(pair_list, replica_ids):
    first_col = pair_list[:, 0]
    second_col = pair_list[:, 1]
    hit_first = replica_ids[:, None] == first_col[None, :]
    hit_second = replica_ids[:, None] == second_col[None, :]
    partner_sum = jnp.sum(jnp.where(hit_first, second_col[None, :], 0), 1) + jnp.sum(
        jnp.where(hit_second, first_col[None, :], 0), 1
    )
    listed = jnp.any(hit_first, 1) | jnp.any(hit_second, 1)
    return jnp.where(listed, partner_sum, replica_ids)


def exchange(state, swap_pairs):
    count = lax.axis_size("rep")
    rows, width = state.shape
    partner = partner_of(swap_pairs, jnp.arange(count, dtype=jnp.int32))
    chunks = state.reshape(rows, count, width // count).transpose(1, 0, 2)
    spread = lax.all_to_all(chunks, "rep", 0, 0, tiled=True)
    routed = jnp.take(spread, partner, axis=0)
    gathered = lax.all_to_all(routed, "rep", 0, 0, tiled=True)
    return gathered.transpose(1, 0, 2).reshape(rows, width)


def select_table(index_list, width):
    cluster_ids = jnp.arange(width, dtype=jnp.int32)
    return (index_list[:, None] == cluster_ids[None, :]).astype(jnp.float32)


def pair_block(extended, strength_all, charge_all, ham_scale, tile_first, tile_second, live_mask):
    count_tiles = tile_first.shape[0]
    width = extended.shape[1]
    select_first = select_table(tile_first, width)
    select_second = select_table(tile_second, width)
    coords_i = jnp.einsum("te,xec->xct", select_first, extended, precision=exact)
    coords_j = jnp.einsum("te,xec->xtc", select_second, extended, precision=exact)
    offsets = (coords_i[:, :, :, None] - coords_j[:, None, :, :]).reshape(3, CL, count_tiles * CL)
    sq_dist = offsets[0] * offsets[0] + offsets[1] * offsets[1] + offsets[2] * offsets[2]
    params_all = jnp.stack([strength_all, charge_all], 0)
    params_i = jnp.einsum("te,pec->pct", select_first, params_all, precision=exact)
    params_j = jnp.einsum("te,pec->ptc", select_second, params_all, precision=exact)
    strength_prod = (params_i[0][:, :, None] * params_j[0][None, :, :]).reshape(
        CL, count_tiles * CL
    )
    charge_prod = (params_i[1][:, :, None] * params_j[1][None, :, :]).reshape(CL, count_tiles * CL)
    gauss_term = strength_prod * jnp.exp(-sq_dist)
    inv_root = lax.rsqrt(sq_dist + soft_sq)
    coulomb = ham_scale * charge_prod * inv_root
    same_tile = tile_first == tile_second
    weight_tile = jnp.where(live_mask, jnp.where(same_tile, 0.5, 1.0), 0.0).astype(jnp.float32)
    weight_col = jnp.repeat(weight_tile, CL)[None, :]
    slope = gauss_term + 0.5 * coulomb * inv_root * inv_root
    pushes = (2.0 * slope * weight_col)[None, :, :] * offsets
    force_i = pushes.reshape(3, CL, count_tiles, CL).sum(-1)
    force_j = -pushes.sum(1).reshape(3, count_tiles, CL)
    atom_ids = jnp.arange(CL, dtype=jnp.int32)
    column_ids = jnp.arange(count_tiles * CL, dtype=jnp.int32) % CL
    self_pair = jnp.repeat(same_tile, CL)[None, :] & (atom_ids[:, None] == column_ids[None, :])
    energy = jnp.sum(jnp.where(self_pair, 0.0, (gauss_term + coulomb) * weight_col))
    spread_i = jnp.einsum("te,xct->xec", select_first, force_i, precision=exact)
    spread_j = jnp.einsum("te,xtc->xec", select_second, force_j, precision=exact)
    return (spread_i + spread_j, energy)


def local(
    positions,
    velocities,
    inv_mass,
    strength,
    charge,
    scaling,
    tile_pairs,
    tile_counts,
    halo_clusters,
    swap_pairs,
):
    coords = positions[0]
    speeds = velocities[0]
    ham_scale = scaling[0]
    firsts_flat = tile_pairs[0, 0]
    seconds_flat = tile_pairs[0, 1]
    live_count = tile_counts[0, 0]
    halo_index = halo_clusters[0]
    atoms_here = coords.shape[1]
    halo_table = select_table(halo_index, CD)
    params = jnp.stack([strength, charge], 0).reshape(2, CD, CL)
    sent_params = jnp.einsum("hc,pck->phk", halo_table, params, precision=exact).reshape(
        2, HALO * CL
    )
    got_params = from_behind(sent_params, "slab", -1).reshape(2, HALO, CL)
    strength_all = jnp.concatenate([params[0], got_params[0]], 0)
    charge_all = jnp.concatenate([params[1], got_params[1]], 0)
    lift = jnp.array([0.0, 0.0, slab_width], jnp.float32)[:, None]
    param_cols = jnp.stack([strength_all, ham_scale * charge_all], 0)
    param_rows = jnp.stack([as_rows(strength_all), as_rows(charge_all)], 0)
    tile_list = jnp.stack([firsts_flat, seconds_flat], 0)

    def evaluate(coords_now):
        blocks = coords_now.reshape(3, CD, CL)
        sent_coords = jnp.einsum("hc,xck->xhk", halo_table, blocks, precision=exact).reshape(
            3, HALO * CL
        )
        from_above = from_behind(sent_coords, "slab", -1) + lift
        extended = jnp.concatenate([blocks, from_above.reshape(3, HALO, CL)], 1)
        forces, energy = slab_pairs(extended, param_cols, param_rows, tile_list, live_count)
        returned = from_behind(forces[:, CD:].reshape(3, HALO * CL), "slab", 1)
        back_home = jnp.einsum(
            "hc,xhk->xck", halo_table, returned.reshape(3, HALO, CL), precision=exact
        )
        local_forces = forces[:, :CD] + back_home
        return (local_forces.reshape(3, atoms_here), energy)

    def verlet_step(step_idx, carry):
        coords, speeds, forces, energy = carry
        speeds = speeds + half_step * forces * inv_mass
        coords = coords + time_step * speeds
        forces, energy = evaluate(coords)
        speeds = speeds + half_step * forces * inv_mass
        return (coords, speeds, forces, energy)

    forces, energy = evaluate(coords)
    coords, speeds, forces, energy = lax.fori_loop(
        0, STEPS, verlet_step, (coords, speeds, forces, energy)
    )
    total_energy = lax.psum(energy, "slab")
    potential = (total_energy / (atoms_here * lax.axis_size("slab"))).reshape(1)
    state = jnp.concatenate([coords, speeds], 0)
    swapped = exchange(state, swap_pairs)
    return (swapped[:3][None], swapped[3:][None], potential)


def solution(mesh):
    in_specs = (
        P("rep", None, "slab"),
        P("rep", None, "slab"),
        P("slab"),
        P("slab"),
        P("slab"),
        P("rep"),
        P("rep", None, "slab"),
        P("rep", "slab"),
        P("rep", "slab"),
        P(),
    )
    out_specs = (P("rep", None, "slab"), P("rep", None, "slab"), P("rep"))
    return jax.shard_map(local, mesh=mesh, in_specs=in_specs, out_specs=out_specs, check_vma=False)
```

```python
import jax
import jax.numpy as jnp
from jax import lax
from jax.sharding import PartitionSpec as P
from jax.experimental import pallas as pl
from jax.experimental.pallas import tpu as pltpu

CL = 64
CD = 64
STEPS = 4
HALO = 16
NT_MAX = 192
HALF = CL // 2


tile_block = 16
time_step = 0.04
half_step = 0.02
soft_sq = 0.25
slab_width = 2.0
exact = lax.Precision.HIGHEST


def spread_masks():
    rows = lax.broadcasted_iota(jnp.int32, (HALF, CL), 0)
    atoms = lax.broadcasted_iota(jnp.int32, (HALF, CL), 1)
    pick = (atoms // 2 == rows).astype(jnp.float32)
    atoms_t = lax.broadcasted_iota(jnp.int32, (CL, 2 * CL), 0)
    lanes_t = lax.broadcasted_iota(jnp.int32, (CL, 2 * CL), 1)
    place = (atoms_t % 2 == lanes_t // CL).astype(jnp.float32)
    return pick, place


def to_columns(values, pick, place):
    width = values.shape[0]
    picked = (values[:, None, :] * pick[None]).reshape(width * HALF, CL)
    place_b = place.astype(jnp.bfloat16)
    hi = picked.astype(jnp.bfloat16)
    rest = picked - hi.astype(jnp.float32)
    mid = rest.astype(jnp.bfloat16)
    lo = (rest - mid.astype(jnp.float32)).astype(jnp.bfloat16)
    spread = jnp.dot(hi, place_b, preferred_element_type=jnp.float32)
    spread = spread + jnp.dot(mid, place_b, preferred_element_type=jnp.float32)
    spread = spread + jnp.dot(lo, place_b, preferred_element_type=jnp.float32)
    return spread.reshape(width, HALF, 2 * CL)


def from_columns(blocks, pick, place):
    width = blocks.shape[0]
    folded = lax.dot_general(
        blocks.reshape(width * HALF, 2 * CL), place, (((1,), (1,)), ((), ())),
        precision=exact, preferred_element_type=jnp.float32,
    )
    return jnp.sum(folded.reshape(width, HALF, CL) * pick[None], axis=1)


def pair_kernel(tiles_ref, count_ref, ext_ref, prm_ref, xrow_ref, prow_ref,
                fi_ref, frow_ref, en_ref, xcol_ref, pcol_ref, fcol_ref):
    pick, place = spread_masks()
    for c in range(3):
        xcol_ref[c] = to_columns(ext_ref[c], pick, place)
    for c in range(2):
        pcol_ref[c] = to_columns(prm_ref[c], pick, place)
    fcol_ref[...] = jnp.zeros(fcol_ref.shape, jnp.float32)
    frow_ref[...] = jnp.zeros(frow_ref.shape, jnp.float32)
    rows = lax.broadcasted_iota(jnp.int32, (HALF, 2 * CL), 0)
    lanes = lax.broadcasted_iota(jnp.int32, (HALF, 2 * CL), 1)
    w_same = jnp.where(2 * rows + lanes // CL == lanes % CL, 0.0, 0.5).astype(jnp.float32)

    def body(t, acc):
        i = tiles_ref[0, t]
        j = tiles_ref[1, t]
        dx = xcol_ref[0, i] - xrow_ref[0, j]
        dy = xcol_ref[1, i] - xrow_ref[1, j]
        dz = xcol_ref[2, i] - xrow_ref[2, j]
        sq = dx * dx + dy * dy + dz * dz
        gauss = pcol_ref[0, i] * prow_ref[0, j] * jnp.exp(-sq)
        inv_root = lax.rsqrt(sq + soft_sq)
        coulomb = pcol_ref[1, i] * prow_ref[1, j] * inv_root
        same = i == j
        w_force = jnp.where(same, 0.5, 1.0).astype(jnp.float32)
        w_energy = jnp.where(same, w_same, 1.0)
        slope = w_force * (2.0 * gauss + coulomb * inv_root * inv_root)
        px = slope * dx
        py = slope * dy
        pz = slope * dz
        fcol_ref[0, i] += px
        fcol_ref[1, i] += py
        fcol_ref[2, i] += pz
        frow_ref[0, j] -= jnp.sum(px, axis=0, keepdims=True)
        frow_ref[1, j] -= jnp.sum(py, axis=0, keepdims=True)
        frow_ref[2, j] -= jnp.sum(pz, axis=0, keepdims=True)
        return acc + w_energy * (gauss + coulomb)

    acc = lax.fori_loop(0, count_ref[0], body, jnp.zeros((HALF, 2 * CL), jnp.float32))
    en_ref[...] = acc
    for c in range(3):
        fi_ref[c] = from_columns(fcol_ref[c], pick, place)


def as_rows(values):
    lead = values.shape[:-1]
    return jnp.concatenate([values, values], -1).reshape(lead + (1, 2 * CL))


def slab_pairs(extended, prm_cols, prow, tiles, count):
    width = extended.shape[1]
    xrow = as_rows(extended)
    smem = pl.BlockSpec(memory_space=pltpu.SMEM)
    vmem = pl.BlockSpec(memory_space=pltpu.VMEM)
    f_i, frow, acc = pl.pallas_call(
        pair_kernel,
        out_shape=(
            jax.ShapeDtypeStruct((3, width, CL), jnp.float32),
            jax.ShapeDtypeStruct((3, width, 1, 2 * CL), jnp.float32),
            jax.ShapeDtypeStruct((HALF, 2 * CL), jnp.float32),
        ),
        in_specs=[smem, smem, vmem, vmem, vmem, vmem],
        out_specs=(vmem, vmem, vmem),
        scratch_shapes=[
            pltpu.VMEM((3, width, HALF, 2 * CL), jnp.float32),
            pltpu.VMEM((2, width, HALF, 2 * CL), jnp.float32),
            pltpu.VMEM((3, width, HALF, 2 * CL), jnp.float32),
        ],
        compiler_params=pltpu.CompilerParams(vmem_limit_bytes=48 * 1024 * 1024),
    )(tiles, count.reshape(1), extended, prm_cols, xrow, prow)
    f_j = frow.reshape(3, width, 2, CL).sum(2)
    return f_i + f_j, jnp.sum(acc)


def from_behind(value, axis, steps):
    count = lax.axis_size(axis)
    pairs = [(source, (source + steps) % count) for source in range(count)]
    return lax.ppermute(value, axis, pairs)


def partner_of(pair_list, replica_ids):
    first_col = pair_list[:, 0]
    second_col = pair_list[:, 1]
    hit_first = replica_ids[:, None] == first_col[None, :]
    hit_second = replica_ids[:, None] == second_col[None, :]
    partner_sum = jnp.sum(jnp.where(hit_first, second_col[None, :], 0), 1) + jnp.sum(
        jnp.where(hit_second, first_col[None, :], 0), 1
    )
    listed = jnp.any(hit_first, 1) | jnp.any(hit_second, 1)
    return jnp.where(listed, partner_sum, replica_ids)


def exchange(state, swap_pairs):
    count = lax.axis_size("rep")
    rows, width = state.shape
    partner = partner_of(swap_pairs, jnp.arange(count, dtype=jnp.int32))
    chunks = state.reshape(rows, count, width // count).transpose(1, 0, 2)
    spread = lax.all_to_all(chunks, "rep", 0, 0, tiled=True)
    routed = jnp.take(spread, partner, axis=0)
    gathered = lax.all_to_all(routed, "rep", 0, 0, tiled=True)
    return gathered.transpose(1, 0, 2).reshape(rows, width)


def select_table(index_list, width):
    cluster_ids = jnp.arange(width, dtype=jnp.int32)
    return (index_list[:, None] == cluster_ids[None, :]).astype(jnp.float32)


def local(
    positions,
    velocities,
    inv_mass,
    strength,
    charge,
    scaling,
    tile_pairs,
    tile_counts,
    halo_clusters,
    swap_pairs,
):
    ham_scale = scaling[0]
    tile_list = tile_pairs[0]
    live_count = tile_counts[0, 0]
    halo_index = halo_clusters[0]
    atoms_here = positions.shape[2]
    own = jnp.concatenate(
        [
            positions[0].reshape(3, CD, CL),
            velocities[0].reshape(3, CD, CL),
            jnp.stack([inv_mass, strength, charge], 0).reshape(3, CD, CL),
        ],
        0,
    )
    sent = jnp.take(own, halo_index, axis=1)
    got = from_behind(sent, "slab", -1)
    full = jnp.concatenate([own, got], 1)
    coords = full[0:3]
    speeds = full[3:6]
    inv_mass_all = full[6]
    strength_all = full[7]
    charge_all = full[8]
    cluster_ids = lax.broadcasted_iota(jnp.int32, (3, CD + HALO, CL), 1)
    lift_all = jnp.where(
        (cluster_ids >= CD) & (lax.broadcasted_iota(jnp.int32, (3, CD + HALO, CL), 0) == 2),
        slab_width,
        0.0,
    ).astype(jnp.float32)
    param_cols = jnp.stack([strength_all, ham_scale * charge_all], 0)
    param_rows = jnp.stack([as_rows(strength_all), as_rows(charge_all)], 0)
    halo_table = select_table(halo_index, CD)

    def evaluate(coords_now):
        extended = coords_now + lift_all
        forces, energy = slab_pairs(extended, param_cols, param_rows, tile_list, live_count)
        owned_part = jnp.take(forces[:, :CD], halo_index, axis=1)
        returned = from_behind(forces[:, CD:], "slab", 1)
        from_owner = from_behind(owned_part, "slab", -1)
        back_home = jnp.einsum("hc,xhk->xck", halo_table, returned, precision=exact)
        total = jnp.concatenate([forces[:, :CD] + back_home, forces[:, CD:] + from_owner], 1)
        return (total, energy)

    def verlet_step(step_idx, carry):
        coords, speeds, forces, energy = carry
        speeds = speeds + half_step * forces * inv_mass_all
        coords = coords + time_step * speeds
        forces, energy = evaluate(coords)
        speeds = speeds + half_step * forces * inv_mass_all
        return (coords, speeds, forces, energy)

    forces, energy = evaluate(coords)
    coords, speeds, forces, energy = lax.fori_loop(
        0, STEPS, verlet_step, (coords, speeds, forces, energy)
    )
    total_energy = slab_sum(energy)
    potential = (total_energy / (atoms_here * lax.axis_size("slab"))).reshape(1)
    state = jnp.concatenate(
        [coords[:, :CD].reshape(3, atoms_here), speeds[:, :CD].reshape(3, atoms_here)], 0
    )
    swapped = exchange(state, swap_pairs)
    return (swapped[:3][None], swapped[3:][None], potential)


def slab_sum(value):
    count = lax.axis_size("slab")
    stride = 1
    while stride < count:
        pairs = [(source, source ^ stride) for source in range(count)]
        value = value + lax.ppermute(value, "slab", pairs)
        stride *= 2
    return value


def solution(mesh):
    in_specs = (
        P("rep", None, "slab"),
        P("rep", None, "slab"),
        P("slab"),
        P("slab"),
        P("slab"),
        P("rep"),
        P("rep", None, "slab"),
        P("rep", "slab"),
        P("rep", "slab"),
        P(),
    )
    out_specs = (P("rep", None, "slab"), P("rep", None, "slab"), P("rep"))
    return jax.shard_map(local, mesh=mesh, in_specs=in_specs, out_specs=out_specs, check_vma=False)
```

```python
import jax
import jax.numpy as jnp
from jax import lax
from jax.sharding import PartitionSpec as P
from jax.experimental import pallas as pl
from jax.experimental.pallas import tpu as pltpu

CL = 64
CD = 64
STEPS = 4
HALO = 16
NT_MAX = 192
HALF = CL // 2


tile_block = 16
time_step = 0.04
half_step = 0.02
soft_sq = 0.25
slab_width = 2.0
exact = lax.Precision.HIGHEST


def spread_masks():
    rows = lax.broadcasted_iota(jnp.int32, (HALF, CL), 0)
    atoms = lax.broadcasted_iota(jnp.int32, (HALF, CL), 1)
    pick = (atoms // 2 == rows).astype(jnp.float32)
    atoms_t = lax.broadcasted_iota(jnp.int32, (CL, 2 * CL), 0)
    lanes_t = lax.broadcasted_iota(jnp.int32, (CL, 2 * CL), 1)
    place = (atoms_t % 2 == lanes_t // CL).astype(jnp.float32)
    twice = (atoms_t == lanes_t % CL).astype(jnp.float32)
    return pick, place, twice


def split_dot(values, matrix, dims):
    matrix_b = matrix.astype(jnp.bfloat16)
    hi = values.astype(jnp.bfloat16)
    rest = values - hi.astype(jnp.float32)
    mid = rest.astype(jnp.bfloat16)
    lo = (rest - mid.astype(jnp.float32)).astype(jnp.bfloat16)
    total = None
    for part in (hi, mid, lo):
        term = lax.dot_general(part, matrix_b, (dims, ((), ())), preferred_element_type=jnp.float32)
        total = term if total is None else total + term
    return total


def to_columns(values, pick, place):
    width = values.shape[0]
    picked = (values[:, None, :] * pick[None]).reshape(width * HALF, CL)
    spread = split_dot(picked, place, ((1,), (0,)))
    return spread.reshape(width, HALF, 2 * CL)


def from_columns(blocks, pick, place):
    width = blocks.shape[0]
    folded = lax.dot_general(
        blocks.reshape(width * HALF, 2 * CL), place, (((1,), (1,)), ((), ())),
        precision=exact, preferred_element_type=jnp.float32,
    )
    return jnp.sum(folded.reshape(width, HALF, CL) * pick[None], axis=1)


def pair_kernel(tiles_ref, count_ref, ext_ref, prm_ref, force_ref, en_ref,
                xcol_ref, pcol_ref, xrow_ref, prow_ref, fcol_ref, frow_ref):
    pick, place, twice = spread_masks()
    for c in range(3):
        xcol_ref[c] = to_columns(ext_ref[c], pick, place)
        xrow_ref[c] = split_dot(ext_ref[c], twice, ((1,), (0,)))
    for c in range(2):
        pcol_ref[c] = to_columns(prm_ref[c], pick, place)
        prow_ref[c] = split_dot(prm_ref[2 * c], twice, ((1,), (0,)))
    fcol_ref[...] = jnp.zeros(fcol_ref.shape, jnp.float32)
    frow_ref[...] = jnp.zeros(frow_ref.shape, jnp.float32)
    rows = lax.broadcasted_iota(jnp.int32, (HALF, 2 * CL), 0)
    lanes = lax.broadcasted_iota(jnp.int32, (HALF, 2 * CL), 1)
    w_same = jnp.where(2 * rows + lanes // CL == lanes % CL, 0.0, 0.5).astype(jnp.float32)

    def body(t, acc):
        i = tiles_ref[0, t]
        j = tiles_ref[1, t]
        row = pl.ds(j, 1)
        dx = xcol_ref[0, i] - xrow_ref[0, row, :]
        dy = xcol_ref[1, i] - xrow_ref[1, row, :]
        dz = xcol_ref[2, i] - xrow_ref[2, row, :]
        sq = dx * dx + dy * dy + dz * dz
        gauss = pcol_ref[0, i] * prow_ref[0, row, :] * jnp.exp(-sq)
        inv_root = lax.rsqrt(sq + soft_sq)
        coulomb = pcol_ref[1, i] * prow_ref[1, row, :] * inv_root
        same = i == j
        w_force = jnp.where(same, 0.5, 1.0).astype(jnp.float32)
        w_energy = jnp.where(same, w_same, 1.0)
        slope = w_force * (2.0 * gauss + coulomb * inv_root * inv_root)
        px = slope * dx
        py = slope * dy
        pz = slope * dz
        fcol_ref[0, i] += px
        fcol_ref[1, i] += py
        fcol_ref[2, i] += pz
        frow_ref[0, row, :] -= jnp.sum(px, axis=0, keepdims=True)
        frow_ref[1, row, :] -= jnp.sum(py, axis=0, keepdims=True)
        frow_ref[2, row, :] -= jnp.sum(pz, axis=0, keepdims=True)
        return acc + w_energy * (gauss + coulomb)

    acc = lax.fori_loop(0, count_ref[0], body, jnp.zeros((HALF, 2 * CL), jnp.float32))
    en_ref[...] = acc
    for c in range(3):
        f_j = lax.dot_general(
            frow_ref[c], twice, (((1,), (1,)), ((), ())),
            precision=exact, preferred_element_type=jnp.float32,
        )
        force_ref[c] = from_columns(fcol_ref[c], pick, place) + f_j


def slab_pairs(extended, prm, tiles, count):
    width = extended.shape[1]
    smem = pl.BlockSpec(memory_space=pltpu.SMEM)
    vmem = pl.BlockSpec(memory_space=pltpu.VMEM)
    forces, acc = pl.pallas_call(
        pair_kernel,
        out_shape=(
            jax.ShapeDtypeStruct((3, width, CL), jnp.float32),
            jax.ShapeDtypeStruct((HALF, 2 * CL), jnp.float32),
        ),
        in_specs=[smem, smem, vmem, vmem],
        out_specs=(vmem, vmem),
        scratch_shapes=[
            pltpu.VMEM((3, width, HALF, 2 * CL), jnp.float32),
            pltpu.VMEM((2, width, HALF, 2 * CL), jnp.float32),
            pltpu.VMEM((3, width, 2 * CL), jnp.float32),
            pltpu.VMEM((2, width, 2 * CL), jnp.float32),
            pltpu.VMEM((3, width, HALF, 2 * CL), jnp.float32),
            pltpu.VMEM((3, width, 2 * CL), jnp.float32),
        ],
        compiler_params=pltpu.CompilerParams(vmem_limit_bytes=48 * 1024 * 1024),
    )(tiles, count.reshape(1), extended, prm)
    return forces, jnp.sum(acc)


def from_behind(value, axis, steps):
    count = lax.axis_size(axis)
    pairs = [(source, (source + steps) % count) for source in range(count)]
    return lax.ppermute(value, axis, pairs)


def partner_of(pair_list, replica_ids):
    first_col = pair_list[:, 0]
    second_col = pair_list[:, 1]
    hit_first = replica_ids[:, None] == first_col[None, :]
    hit_second = replica_ids[:, None] == second_col[None, :]
    partner_sum = jnp.sum(jnp.where(hit_first, second_col[None, :], 0), 1) + jnp.sum(
        jnp.where(hit_second, first_col[None, :], 0), 1
    )
    listed = jnp.any(hit_first, 1) | jnp.any(hit_second, 1)
    return jnp.where(listed, partner_sum, replica_ids)


def exchange(state, swap_pairs):
    count = lax.axis_size("rep")
    rows, width = state.shape
    partner = partner_of(swap_pairs, jnp.arange(count, dtype=jnp.int32))
    chunks = state.reshape(rows, count, width // count).transpose(1, 0, 2)
    spread = lax.all_to_all(chunks, "rep", 0, 0, tiled=True)
    routed = jnp.take(spread, partner, axis=0)
    gathered = lax.all_to_all(routed, "rep", 0, 0, tiled=True)
    return gathered.transpose(1, 0, 2).reshape(rows, width)


def select_table(index_list, width):
    cluster_ids = jnp.arange(width, dtype=jnp.int32)
    return (index_list[:, None] == cluster_ids[None, :]).astype(jnp.float32)


def pair_block(extended, strength_all, charge_all, ham_scale, tile_first, tile_second, live_mask):
    count_tiles = tile_first.shape[0]
    width = extended.shape[1]
    select_first = select_table(tile_first, width)
    select_second = select_table(tile_second, width)
    coords_i = jnp.einsum("te,xec->xct", select_first, extended, precision=exact)
    coords_j = jnp.einsum("te,xec->xtc", select_second, extended, precision=exact)
    offsets = (coords_i[:, :, :, None] - coords_j[:, None, :, :]).reshape(3, CL, count_tiles * CL)
    sq_dist = offsets[0] * offsets[0] + offsets[1] * offsets[1] + offsets[2] * offsets[2]
    params_all = jnp.stack([strength_all, charge_all], 0)
    params_i = jnp.einsum("te,pec->pct", select_first, params_all, precision=exact)
    params_j = jnp.einsum("te,pec->ptc", select_second, params_all, precision=exact)
    strength_prod = (params_i[0][:, :, None] * params_j[0][None, :, :]).reshape(
        CL, count_tiles * CL
    )
    charge_prod = (params_i[1][:, :, None] * params_j[1][None, :, :]).reshape(CL, count_tiles * CL)
    gauss_term = strength_prod * jnp.exp(-sq_dist)
    inv_root = lax.rsqrt(sq_dist + soft_sq)
    coulomb = ham_scale * charge_prod * inv_root
    same_tile = tile_first == tile_second
    weight_tile = jnp.where(live_mask, jnp.where(same_tile, 0.5, 1.0), 0.0).astype(jnp.float32)
    weight_col = jnp.repeat(weight_tile, CL)[None, :]
    slope = gauss_term + 0.5 * coulomb * inv_root * inv_root
    pushes = (2.0 * slope * weight_col)[None, :, :] * offsets
    force_i = pushes.reshape(3, CL, count_tiles, CL).sum(-1)
    force_j = -pushes.sum(1).reshape(3, count_tiles, CL)
    atom_ids = jnp.arange(CL, dtype=jnp.int32)
    column_ids = jnp.arange(count_tiles * CL, dtype=jnp.int32) % CL
    self_pair = jnp.repeat(same_tile, CL)[None, :] & (atom_ids[:, None] == column_ids[None, :])
    energy = jnp.sum(jnp.where(self_pair, 0.0, (gauss_term + coulomb) * weight_col))
    spread_i = jnp.einsum("te,xct->xec", select_first, force_i, precision=exact)
    spread_j = jnp.einsum("te,xtc->xec", select_second, force_j, precision=exact)
    return (spread_i + spread_j, energy)


def local(
    positions,
    velocities,
    inv_mass,
    strength,
    charge,
    scaling,
    tile_pairs,
    tile_counts,
    halo_clusters,
    swap_pairs,
):
    coords = positions[0]
    speeds = velocities[0]
    ham_scale = scaling[0]
    firsts_flat = tile_pairs[0, 0]
    seconds_flat = tile_pairs[0, 1]
    live_count = tile_counts[0, 0]
    halo_index = halo_clusters[0]
    atoms_here = coords.shape[1]
    halo_table = select_table(halo_index, CD)
    params = jnp.stack([strength, charge], 0).reshape(2, CD, CL)
    sent_params = jnp.einsum("hc,pck->phk", halo_table, params, precision=exact).reshape(
        2, HALO * CL
    )
    got_params = from_behind(sent_params, "slab", -1).reshape(2, HALO, CL)
    strength_all = jnp.concatenate([params[0], got_params[0]], 0)
    charge_all = jnp.concatenate([params[1], got_params[1]], 0)
    lift = jnp.array([0.0, 0.0, slab_width], jnp.float32)[:, None]
    param_all = jnp.stack([strength_all, ham_scale * charge_all, charge_all], 0)
    tile_list = jnp.stack([firsts_flat, seconds_flat], 0)

    def evaluate(coords_now):
        blocks = coords_now.reshape(3, CD, CL)
        sent_coords = jnp.einsum("hc,xck->xhk", halo_table, blocks, precision=exact).reshape(
            3, HALO * CL
        )
        from_above = from_behind(sent_coords, "slab", -1) + lift
        extended = jnp.concatenate([blocks, from_above.reshape(3, HALO, CL)], 1)
        forces, energy = slab_pairs(extended, param_all, tile_list, live_count)
        returned = from_behind(forces[:, CD:].reshape(3, HALO * CL), "slab", 1)
        back_home = jnp.einsum(
            "hc,xhk->xck", halo_table, returned.reshape(3, HALO, CL), precision=exact
        )
        local_forces = forces[:, :CD] + back_home
        return (local_forces.reshape(3, atoms_here), energy)

    def verlet_step(step_idx, carry):
        coords, speeds, forces, energy = carry
        speeds = speeds + half_step * forces * inv_mass
        coords = coords + time_step * speeds
        forces, energy = evaluate(coords)
        speeds = speeds + half_step * forces * inv_mass
        return (coords, speeds, forces, energy)

    forces, energy = evaluate(coords)
    coords, speeds, forces, energy = lax.fori_loop(
        0, STEPS, verlet_step, (coords, speeds, forces, energy)
    )
    total_energy = lax.psum(energy, "slab")
    potential = (total_energy / (atoms_here * lax.axis_size("slab"))).reshape(1)
    state = jnp.concatenate([coords, speeds], 0)
    swapped = exchange(state, swap_pairs)
    return (swapped[:3][None], swapped[3:][None], potential)


def solution(mesh):
    in_specs = (
        P("rep", None, "slab"),
        P("rep", None, "slab"),
        P("slab"),
        P("slab"),
        P("slab"),
        P("rep"),
        P("rep", None, "slab"),
        P("rep", "slab"),
        P("rep", "slab"),
        P(),
    )
    out_specs = (P("rep", None, "slab"), P("rep", None, "slab"), P("rep"))
    return jax.shard_map(local, mesh=mesh, in_specs=in_specs, out_specs=out_specs, check_vma=False)
```

```python
import jax
import jax.numpy as jnp
from jax import lax
from jax.sharding import PartitionSpec as P
from jax.experimental import pallas as pl
from jax.experimental.pallas import tpu as pltpu

CL = 64
CD = 64
STEPS = 4
HALO = 16
NT_MAX = 192
HALF = CL // 2


tile_block = 16
time_step = 0.04
half_step = 0.02
soft_sq = 0.25
slab_width = 2.0
exact = lax.Precision.HIGHEST


def spread_masks():
    rows = lax.broadcasted_iota(jnp.int32, (HALF, CL), 0)
    atoms = lax.broadcasted_iota(jnp.int32, (HALF, CL), 1)
    pick = (atoms // 2 == rows).astype(jnp.float32)
    atoms_t = lax.broadcasted_iota(jnp.int32, (CL, 2 * CL), 0)
    lanes_t = lax.broadcasted_iota(jnp.int32, (CL, 2 * CL), 1)
    place = (atoms_t % 2 == lanes_t // CL).astype(jnp.float32)
    twice = (atoms_t == lanes_t % CL).astype(jnp.float32)
    return pick, place, twice


def split_dot(values, matrix, dims):
    matrix_b = matrix.astype(jnp.bfloat16)
    hi = values.astype(jnp.bfloat16)
    rest = values - hi.astype(jnp.float32)
    mid = rest.astype(jnp.bfloat16)
    lo = (rest - mid.astype(jnp.float32)).astype(jnp.bfloat16)
    total = None
    for part in (hi, mid, lo):
        term = lax.dot_general(part, matrix_b, (dims, ((), ())), preferred_element_type=jnp.float32)
        total = term if total is None else total + term
    return total


def to_columns(values, pick, place):
    width = values.shape[0]
    picked = (values[:, None, :] * pick[None]).reshape(width * HALF, CL)
    spread = split_dot(picked, place, ((1,), (0,)))
    return spread.reshape(width, HALF, 2 * CL)


def from_columns(blocks, pick, place):
    width = blocks.shape[0]
    folded = lax.dot_general(
        blocks.reshape(width * HALF, 2 * CL), place, (((1,), (1,)), ((), ())),
        precision=exact, preferred_element_type=jnp.float32,
    )
    return jnp.sum(folded.reshape(width, HALF, CL) * pick[None], axis=1)


def pair_kernel(tiles_ref, count_ref, ext_ref, prm_ref, force_ref, en_ref,
                xcol_ref, pcol_ref, xrow_ref, prow_ref, fcol_ref, frow_ref):
    pick, place, twice = spread_masks()
    owned = xcol_ref.shape[1]
    for c in range(3):
        xcol_ref[c] = to_columns(ext_ref[c, :owned], pick, place)
        xrow_ref[c] = split_dot(ext_ref[c], twice, ((1,), (0,)))
    for c in range(2):
        pcol_ref[c] = to_columns(prm_ref[c, :owned], pick, place)
        prow_ref[c] = split_dot(prm_ref[2 * c], twice, ((1,), (0,)))
    fcol_ref[...] = jnp.zeros(fcol_ref.shape, jnp.float32)
    frow_ref[...] = jnp.zeros(frow_ref.shape, jnp.float32)
    rows = lax.broadcasted_iota(jnp.int32, (HALF, 2 * CL), 0)
    lanes = lax.broadcasted_iota(jnp.int32, (HALF, 2 * CL), 1)
    w_same = jnp.where(2 * rows + lanes // CL == lanes % CL, 0.0, 0.5).astype(jnp.float32)

    def body(t, acc):
        i = tiles_ref[0, t]
        j = tiles_ref[1, t]
        row = pl.ds(j, 1)
        dx = xcol_ref[0, i] - xrow_ref[0, row, :]
        dy = xcol_ref[1, i] - xrow_ref[1, row, :]
        dz = xcol_ref[2, i] - xrow_ref[2, row, :]
        sq = dx * dx + dy * dy + dz * dz
        gauss = pcol_ref[0, i] * prow_ref[0, row, :] * jnp.exp(-sq)
        inv_root = lax.rsqrt(sq + soft_sq)
        coulomb = pcol_ref[1, i] * prow_ref[1, row, :] * inv_root
        same = i == j
        w_force = jnp.where(same, 0.5, 1.0).astype(jnp.float32)
        w_energy = jnp.where(same, w_same, 1.0)
        slope = w_force * (2.0 * gauss + coulomb * inv_root * inv_root)
        px = slope * dx
        py = slope * dy
        pz = slope * dz
        fcol_ref[0, i] += px
        fcol_ref[1, i] += py
        fcol_ref[2, i] += pz
        frow_ref[0, row, :] -= jnp.sum(px, axis=0, keepdims=True)
        frow_ref[1, row, :] -= jnp.sum(py, axis=0, keepdims=True)
        frow_ref[2, row, :] -= jnp.sum(pz, axis=0, keepdims=True)
        return acc + w_energy * (gauss + coulomb)

    acc = lax.fori_loop(0, count_ref[0], body, jnp.zeros((HALF, 2 * CL), jnp.float32))
    en_ref[...] = acc
    for c in range(3):
        f_j = lax.dot_general(
            frow_ref[c], twice, (((1,), (1,)), ((), ())),
            precision=exact, preferred_element_type=jnp.float32,
        )
        force_ref[c, :owned] = from_columns(fcol_ref[c], pick, place) + f_j[:owned]
        force_ref[c, owned:] = f_j[owned:]


def slab_pairs(extended, prm, tiles, count):
    width = extended.shape[1]
    smem = pl.BlockSpec(memory_space=pltpu.SMEM)
    vmem = pl.BlockSpec(memory_space=pltpu.VMEM)
    forces, acc = pl.pallas_call(
        pair_kernel,
        out_shape=(
            jax.ShapeDtypeStruct((3, width, CL), jnp.float32),
            jax.ShapeDtypeStruct((HALF, 2 * CL), jnp.float32),
        ),
        in_specs=[smem, smem, vmem, vmem],
        out_specs=(vmem, vmem),
        scratch_shapes=[
            pltpu.VMEM((3, CD, HALF, 2 * CL), jnp.float32),
            pltpu.VMEM((2, CD, HALF, 2 * CL), jnp.float32),
            pltpu.VMEM((3, width, 2 * CL), jnp.float32),
            pltpu.VMEM((2, width, 2 * CL), jnp.float32),
            pltpu.VMEM((3, CD, HALF, 2 * CL), jnp.float32),
            pltpu.VMEM((3, width, 2 * CL), jnp.float32),
        ],
        compiler_params=pltpu.CompilerParams(vmem_limit_bytes=48 * 1024 * 1024),
    )(tiles, count.reshape(1), extended, prm)
    return forces, jnp.sum(acc)


def from_behind(value, axis, steps):
    count = lax.axis_size(axis)
    pairs = [(source, (source + steps) % count) for source in range(count)]
    return lax.ppermute(value, axis, pairs)


def partner_of(pair_list, replica_ids):
    first_col = pair_list[:, 0]
    second_col = pair_list[:, 1]
    hit_first = replica_ids[:, None] == first_col[None, :]
    hit_second = replica_ids[:, None] == second_col[None, :]
    partner_sum = jnp.sum(jnp.where(hit_first, second_col[None, :], 0), 1) + jnp.sum(
        jnp.where(hit_second, first_col[None, :], 0), 1
    )
    listed = jnp.any(hit_first, 1) | jnp.any(hit_second, 1)
    return jnp.where(listed, partner_sum, replica_ids)


def exchange(state, swap_pairs):
    count = lax.axis_size("rep")
    rows, width = state.shape
    partner = partner_of(swap_pairs, jnp.arange(count, dtype=jnp.int32))
    chunks = state.reshape(rows, count, width // count).transpose(1, 0, 2)
    spread = lax.all_to_all(chunks, "rep", 0, 0, tiled=True)
    routed = jnp.take(spread, partner, axis=0)
    gathered = lax.all_to_all(routed, "rep", 0, 0, tiled=True)
    return gathered.transpose(1, 0, 2).reshape(rows, width)


def select_table(index_list, width):
    cluster_ids = jnp.arange(width, dtype=jnp.int32)
    return (index_list[:, None] == cluster_ids[None, :]).astype(jnp.float32)


def pair_block(extended, strength_all, charge_all, ham_scale, tile_first, tile_second, live_mask):
    count_tiles = tile_first.shape[0]
    width = extended.shape[1]
    select_first = select_table(tile_first, width)
    select_second = select_table(tile_second, width)
    coords_i = jnp.einsum("te,xec->xct", select_first, extended, precision=exact)
    coords_j = jnp.einsum("te,xec->xtc", select_second, extended, precision=exact)
    offsets = (coords_i[:, :, :, None] - coords_j[:, None, :, :]).reshape(3, CL, count_tiles * CL)
    sq_dist = offsets[0] * offsets[0] + offsets[1] * offsets[1] + offsets[2] * offsets[2]
    params_all = jnp.stack([strength_all, charge_all], 0)
    params_i = jnp.einsum("te,pec->pct", select_first, params_all, precision=exact)
    params_j = jnp.einsum("te,pec->ptc", select_second, params_all, precision=exact)
    strength_prod = (params_i[0][:, :, None] * params_j[0][None, :, :]).reshape(
        CL, count_tiles * CL
    )
    charge_prod = (params_i[1][:, :, None] * params_j[1][None, :, :]).reshape(CL, count_tiles * CL)
    gauss_term = strength_prod * jnp.exp(-sq_dist)
    inv_root = lax.rsqrt(sq_dist + soft_sq)
    coulomb = ham_scale * charge_prod * inv_root
    same_tile = tile_first == tile_second
    weight_tile = jnp.where(live_mask, jnp.where(same_tile, 0.5, 1.0), 0.0).astype(jnp.float32)
    weight_col = jnp.repeat(weight_tile, CL)[None, :]
    slope = gauss_term + 0.5 * coulomb * inv_root * inv_root
    pushes = (2.0 * slope * weight_col)[None, :, :] * offsets
    force_i = pushes.reshape(3, CL, count_tiles, CL).sum(-1)
    force_j = -pushes.sum(1).reshape(3, count_tiles, CL)
    atom_ids = jnp.arange(CL, dtype=jnp.int32)
    column_ids = jnp.arange(count_tiles * CL, dtype=jnp.int32) % CL
    self_pair = jnp.repeat(same_tile, CL)[None, :] & (atom_ids[:, None] == column_ids[None, :])
    energy = jnp.sum(jnp.where(self_pair, 0.0, (gauss_term + coulomb) * weight_col))
    spread_i = jnp.einsum("te,xct->xec", select_first, force_i, precision=exact)
    spread_j = jnp.einsum("te,xtc->xec", select_second, force_j, precision=exact)
    return (spread_i + spread_j, energy)


def local(
    positions,
    velocities,
    inv_mass,
    strength,
    charge,
    scaling,
    tile_pairs,
    tile_counts,
    halo_clusters,
    swap_pairs,
):
    coords = positions[0]
    speeds = velocities[0]
    ham_scale = scaling[0]
    firsts_flat = tile_pairs[0, 0]
    seconds_flat = tile_pairs[0, 1]
    live_count = tile_counts[0, 0]
    halo_index = halo_clusters[0]
    atoms_here = coords.shape[1]
    halo_table = select_table(halo_index, CD)
    params = jnp.stack([strength, charge], 0).reshape(2, CD, CL)
    sent_params = jnp.einsum("hc,pck->phk", halo_table, params, precision=exact).reshape(
        2, HALO * CL
    )
    got_params = from_behind(sent_params, "slab", -1).reshape(2, HALO, CL)
    strength_all = jnp.concatenate([params[0], got_params[0]], 0)
    charge_all = jnp.concatenate([params[1], got_params[1]], 0)
    lift = jnp.array([0.0, 0.0, slab_width], jnp.float32)[:, None]
    param_all = jnp.stack([strength_all, ham_scale * charge_all, charge_all], 0)
    tile_list = jnp.stack([firsts_flat, seconds_flat], 0)

    def evaluate(coords_now):
        blocks = coords_now.reshape(3, CD, CL)
        sent_coords = jnp.einsum("hc,xck->xhk", halo_table, blocks, precision=exact).reshape(
            3, HALO * CL
        )
        from_above = from_behind(sent_coords, "slab", -1) + lift
        extended = jnp.concatenate([blocks, from_above.reshape(3, HALO, CL)], 1)
        forces, energy = slab_pairs(extended, param_all, tile_list, live_count)
        returned = from_behind(forces[:, CD:].reshape(3, HALO * CL), "slab", 1)
        back_home = jnp.einsum(
            "hc,xhk->xck", halo_table, returned.reshape(3, HALO, CL), precision=exact
        )
        local_forces = forces[:, :CD] + back_home
        return (local_forces.reshape(3, atoms_here), energy)

    def verlet_step(step_idx, carry):
        coords, speeds, forces, energy = carry
        speeds = speeds + half_step * forces * inv_mass
        coords = coords + time_step * speeds
        forces, energy = evaluate(coords)
        speeds = speeds + half_step * forces * inv_mass
        return (coords, speeds, forces, energy)

    forces, energy = evaluate(coords)
    coords, speeds, forces, energy = lax.fori_loop(
        0, STEPS, verlet_step, (coords, speeds, forces, energy)
    )
    total_energy = slab_sum(energy)
    potential = (total_energy / (atoms_here * lax.axis_size("slab"))).reshape(1)
    state = jnp.concatenate([coords, speeds], 0)
    swapped = exchange(state, swap_pairs)
    return (swapped[:3][None], swapped[3:][None], potential)


def slab_sum(value):
    count = lax.axis_size("slab")
    stride = 1
    while stride < count:
        pairs = [(source, source ^ stride) for source in range(count)]
        value = value + lax.ppermute(value, "slab", pairs)
        stride *= 2
    return value


def solution(mesh):
    in_specs = (
        P("rep", None, "slab"),
        P("rep", None, "slab"),
        P("slab"),
        P("slab"),
        P("slab"),
        P("rep"),
        P("rep", None, "slab"),
        P("rep", "slab"),
        P("rep", "slab"),
        P(),
    )
    out_specs = (P("rep", None, "slab"), P("rep", None, "slab"), P("rep"))
    return jax.shard_map(local, mesh=mesh, in_specs=in_specs, out_specs=out_specs, check_vma=False)
```

```python
import jax
import jax.numpy as jnp
from jax import lax
from jax.sharding import PartitionSpec as P
from jax.experimental import pallas as pl
from jax.experimental.pallas import tpu as pltpu

CL = 64
CD = 64
STEPS = 4
HALO = 16
NT_MAX = 192
HALF = CL // 2


tile_block = 16
time_step = 0.04
half_step = 0.02
soft_sq = 0.25
slab_width = 2.0
exact = lax.Precision.HIGHEST


def spread_masks():
    rows = lax.broadcasted_iota(jnp.int32, (HALF, CL), 0)
    atoms = lax.broadcasted_iota(jnp.int32, (HALF, CL), 1)
    pick = (atoms // 2 == rows).astype(jnp.float32)
    atoms_t = lax.broadcasted_iota(jnp.int32, (CL, 2 * CL), 0)
    lanes_t = lax.broadcasted_iota(jnp.int32, (CL, 2 * CL), 1)
    place = (atoms_t % 2 == lanes_t // CL).astype(jnp.float32)
    twice = (atoms_t == lanes_t % CL).astype(jnp.float32)
    return pick, place, twice


def split_dot(values, matrix, dims):
    matrix_b = matrix.astype(jnp.bfloat16)
    hi = values.astype(jnp.bfloat16)
    rest = values - hi.astype(jnp.float32)
    mid = rest.astype(jnp.bfloat16)
    lo = (rest - mid.astype(jnp.float32)).astype(jnp.bfloat16)
    total = None
    for part in (hi, mid, lo):
        term = lax.dot_general(part, matrix_b, (dims, ((), ())), preferred_element_type=jnp.float32)
        total = term if total is None else total + term
    return total


def to_columns(values, pick, place):
    width = values.shape[0]
    picked = (values[:, None, :] * pick[None]).reshape(width * HALF, CL)
    spread = split_dot(picked, place, ((1,), (0,)))
    return spread.reshape(width, HALF, 2 * CL)


def from_columns(blocks, pick, place):
    width = blocks.shape[0]
    folded = lax.dot_general(
        blocks.reshape(width * HALF, 2 * CL), place, (((1,), (1,)), ((), ())),
        precision=exact, preferred_element_type=jnp.float32,
    )
    return jnp.sum(folded.reshape(width, HALF, CL) * pick[None], axis=1)


def pair_kernel(tiles_ref, count_ref, ext_ref, prm_ref, force_ref, en_ref,
                xcol_ref, pcol_ref, xrow_ref, prow_ref, fcol_ref, frow_ref):
    pick, place, twice = spread_masks()
    owned = xcol_ref.shape[1]
    for c in range(3):
        xcol_ref[c] = to_columns(ext_ref[c, :owned], pick, place)
        xrow_ref[c] = split_dot(ext_ref[c], twice, ((1,), (0,)))
    for c in range(2):
        pcol_ref[c] = to_columns(prm_ref[c, :owned], pick, place)
        prow_ref[c] = split_dot(prm_ref[2 * c], twice, ((1,), (0,)))
    fcol_ref[...] = jnp.zeros(fcol_ref.shape, jnp.float32)
    frow_ref[...] = jnp.zeros(frow_ref.shape, jnp.float32)
    rows = lax.broadcasted_iota(jnp.int32, (HALF, 2 * CL), 0)
    lanes = lax.broadcasted_iota(jnp.int32, (HALF, 2 * CL), 1)
    w_same = jnp.where(2 * rows + lanes // CL == lanes % CL, 0.0, 0.5).astype(jnp.float32)

    def body(t, acc):
        i = tiles_ref[0, t]
        j = tiles_ref[1, t]
        row = pl.ds(j, 1)
        dx = xcol_ref[0, i] - xrow_ref[0, row, :]
        dy = xcol_ref[1, i] - xrow_ref[1, row, :]
        dz = xcol_ref[2, i] - xrow_ref[2, row, :]
        sq = dx * dx + dy * dy + dz * dz
        gauss = pcol_ref[0, i] * prow_ref[0, row, :] * jnp.exp(-sq)
        inv_root = lax.rsqrt(sq + soft_sq)
        coulomb = pcol_ref[1, i] * prow_ref[1, row, :] * inv_root
        same = i == j
        w_force = jnp.where(same, 0.5, 1.0).astype(jnp.float32)
        w_energy = jnp.where(same, w_same, 1.0)
        slope = w_force * (2.0 * gauss + coulomb * inv_root * inv_root)
        px = slope * dx
        py = slope * dy
        pz = slope * dz
        fcol_ref[0, i] += px
        fcol_ref[1, i] += py
        fcol_ref[2, i] += pz
        frow_ref[0, row, :] -= jnp.sum(px, axis=0, keepdims=True)
        frow_ref[1, row, :] -= jnp.sum(py, axis=0, keepdims=True)
        frow_ref[2, row, :] -= jnp.sum(pz, axis=0, keepdims=True)
        return acc + w_energy * (gauss + coulomb)

    acc = lax.fori_loop(0, count_ref[0], body, jnp.zeros((HALF, 2 * CL), jnp.float32))
    en_ref[...] = acc
    for c in range(3):
        f_j = lax.dot_general(
            frow_ref[c], twice, (((1,), (1,)), ((), ())),
            precision=exact, preferred_element_type=jnp.float32,
        )
        force_ref[c, :owned] = from_columns(fcol_ref[c], pick, place) + f_j[:owned]
        force_ref[c, owned:] = f_j[owned:]


def slab_pairs(extended, prm, tiles, count):
    width = extended.shape[1]
    smem = pl.BlockSpec(memory_space=pltpu.SMEM)
    vmem = pl.BlockSpec(memory_space=pltpu.VMEM)
    forces, acc = pl.pallas_call(
        pair_kernel,
        out_shape=(
            jax.ShapeDtypeStruct((3, width, CL), jnp.float32),
            jax.ShapeDtypeStruct((HALF, 2 * CL), jnp.float32),
        ),
        in_specs=[smem, smem, vmem, vmem],
        out_specs=(vmem, vmem),
        scratch_shapes=[
            pltpu.VMEM((3, CD, HALF, 2 * CL), jnp.float32),
            pltpu.VMEM((2, CD, HALF, 2 * CL), jnp.float32),
            pltpu.VMEM((3, width, 2 * CL), jnp.float32),
            pltpu.VMEM((2, width, 2 * CL), jnp.float32),
            pltpu.VMEM((3, CD, HALF, 2 * CL), jnp.float32),
            pltpu.VMEM((3, width, 2 * CL), jnp.float32),
        ],
        compiler_params=pltpu.CompilerParams(vmem_limit_bytes=48 * 1024 * 1024),
    )(tiles, count.reshape(1), extended, prm)
    return forces, jnp.sum(acc)


def from_behind(value, axis, steps):
    count = lax.axis_size(axis)
    pairs = [(source, (source + steps) % count) for source in range(count)]
    return lax.ppermute(value, axis, pairs)


def partner_of(pair_list, replica_ids):
    first_col = pair_list[:, 0]
    second_col = pair_list[:, 1]
    hit_first = replica_ids[:, None] == first_col[None, :]
    hit_second = replica_ids[:, None] == second_col[None, :]
    partner_sum = jnp.sum(jnp.where(hit_first, second_col[None, :], 0), 1) + jnp.sum(
        jnp.where(hit_second, first_col[None, :], 0), 1
    )
    listed = jnp.any(hit_first, 1) | jnp.any(hit_second, 1)
    return jnp.where(listed, partner_sum, replica_ids)


def exchange(state, swap_pairs):
    count = lax.axis_size("rep")
    rows, width = state.shape
    partner = partner_of(swap_pairs, jnp.arange(count, dtype=jnp.int32))
    chunks = state.reshape(rows, count, width // count).transpose(1, 0, 2)
    spread = lax.all_to_all(chunks, "rep", 0, 0, tiled=True)
    routed = jnp.take(spread, partner, axis=0)
    gathered = lax.all_to_all(routed, "rep", 0, 0, tiled=True)
    return gathered.transpose(1, 0, 2).reshape(rows, width)


def select_table(index_list, width):
    cluster_ids = jnp.arange(width, dtype=jnp.int32)
    return (index_list[:, None] == cluster_ids[None, :]).astype(jnp.float32)


def pair_block(extended, strength_all, charge_all, ham_scale, tile_first, tile_second, live_mask):
    count_tiles = tile_first.shape[0]
    width = extended.shape[1]
    select_first = select_table(tile_first, width)
    select_second = select_table(tile_second, width)
    coords_i = jnp.einsum("te,xec->xct", select_first, extended, precision=exact)
    coords_j = jnp.einsum("te,xec->xtc", select_second, extended, precision=exact)
    offsets = (coords_i[:, :, :, None] - coords_j[:, None, :, :]).reshape(3, CL, count_tiles * CL)
    sq_dist = offsets[0] * offsets[0] + offsets[1] * offsets[1] + offsets[2] * offsets[2]
    params_all = jnp.stack([strength_all, charge_all], 0)
    params_i = jnp.einsum("te,pec->pct", select_first, params_all, precision=exact)
    params_j = jnp.einsum("te,pec->ptc", select_second, params_all, precision=exact)
    strength_prod = (params_i[0][:, :, None] * params_j[0][None, :, :]).reshape(
        CL, count_tiles * CL
    )
    charge_prod = (params_i[1][:, :, None] * params_j[1][None, :, :]).reshape(CL, count_tiles * CL)
    gauss_term = strength_prod * jnp.exp(-sq_dist)
    inv_root = lax.rsqrt(sq_dist + soft_sq)
    coulomb = ham_scale * charge_prod * inv_root
    same_tile = tile_first == tile_second
    weight_tile = jnp.where(live_mask, jnp.where(same_tile, 0.5, 1.0), 0.0).astype(jnp.float32)
    weight_col = jnp.repeat(weight_tile, CL)[None, :]
    slope = gauss_term + 0.5 * coulomb * inv_root * inv_root
    pushes = (2.0 * slope * weight_col)[None, :, :] * offsets
    force_i = pushes.reshape(3, CL, count_tiles, CL).sum(-1)
    force_j = -pushes.sum(1).reshape(3, count_tiles, CL)
    atom_ids = jnp.arange(CL, dtype=jnp.int32)
    column_ids = jnp.arange(count_tiles * CL, dtype=jnp.int32) % CL
    self_pair = jnp.repeat(same_tile, CL)[None, :] & (atom_ids[:, None] == column_ids[None, :])
    energy = jnp.sum(jnp.where(self_pair, 0.0, (gauss_term + coulomb) * weight_col))
    spread_i = jnp.einsum("te,xct->xec", select_first, force_i, precision=exact)
    spread_j = jnp.einsum("te,xtc->xec", select_second, force_j, precision=exact)
    return (spread_i + spread_j, energy)


def local(
    positions,
    velocities,
    inv_mass,
    strength,
    charge,
    scaling,
    tile_pairs,
    tile_counts,
    halo_clusters,
    swap_pairs,
):
    ham_scale = scaling[0]
    tile_list = tile_pairs[0]
    live_count = tile_counts[0, 0]
    halo_index = halo_clusters[0]
    atoms_here = positions.shape[2]
    own = jnp.concatenate(
        [
            positions[0].reshape(3, CD, CL),
            velocities[0].reshape(3, CD, CL),
            jnp.stack([inv_mass, strength, charge], 0).reshape(3, CD, CL),
        ],
        0,
    )
    sent = jnp.take(own, halo_index, axis=1)
    got = from_behind(sent, "slab", -1)
    full = jnp.concatenate([own, got], 1)
    coords = full[0:3]
    speeds = full[3:6]
    inv_mass_all = full[6]
    strength_all = full[7]
    charge_all = full[8]
    cluster_ids = lax.broadcasted_iota(jnp.int32, (3, CD + HALO, CL), 1)
    lift_all = jnp.where(
        (cluster_ids >= CD) & (lax.broadcasted_iota(jnp.int32, (3, CD + HALO, CL), 0) == 2),
        slab_width,
        0.0,
    ).astype(jnp.float32)
    param_all = jnp.stack([strength_all, ham_scale * charge_all, charge_all], 0)
    halo_table = select_table(halo_index, CD)

    def evaluate(coords_now):
        extended = coords_now + lift_all
        forces, energy = slab_pairs(extended, param_all, tile_list, live_count)
        owned_part = jnp.take(forces[:, :CD], halo_index, axis=1)
        returned, from_owner = trade_halo(forces[:, CD:], owned_part)
        back_home = jnp.einsum("hc,xhk->xck", halo_table, returned, precision=exact)
        total = jnp.concatenate([forces[:, :CD] + back_home, forces[:, CD:] + from_owner], 1)
        return (total, energy)

    def verlet_step(step_idx, carry):
        coords, speeds, forces, energy = carry
        speeds = speeds + half_step * forces * inv_mass_all
        coords = coords + time_step * speeds
        forces, energy = evaluate(coords)
        speeds = speeds + half_step * forces * inv_mass_all
        return (coords, speeds, forces, energy)

    forces, energy = evaluate(coords)
    coords, speeds, forces, energy = lax.fori_loop(
        0, STEPS, verlet_step, (coords, speeds, forces, energy)
    )
    total_energy = slab_sum(energy)
    potential = (total_energy / (atoms_here * lax.axis_size("slab"))).reshape(1)
    state = jnp.concatenate(
        [coords[:, :CD].reshape(3, atoms_here), speeds[:, :CD].reshape(3, atoms_here)], 0
    )
    swapped = exchange(state, swap_pairs)
    return (swapped[:3][None], swapped[3:][None], potential)


def trade_halo(up_part, down_part):
    count = lax.axis_size("slab")
    if count < 3:
        return (from_behind(up_part, "slab", 1), from_behind(down_part, "slab", -1))
    me = lax.axis_index("slab")
    above = (me + 1) % count
    below = (me - 1) % count
    slots = jnp.arange(count, dtype=jnp.int32).reshape((count,) + (1,) * up_part.ndim)
    payload = jnp.where(slots == above, up_part[None], jnp.where(slots == below, down_part[None], 0.0))
    got = lax.all_to_all(payload, "slab", 0, 0, tiled=True)
    return (jnp.take(got, below, axis=0), jnp.take(got, above, axis=0))


def slab_sum(value):
    count = lax.axis_size("slab")
    stride = 1
    while stride < count:
        pairs = [(source, source ^ stride) for source in range(count)]
        value = value + lax.ppermute(value, "slab", pairs)
        stride *= 2
    return value


def solution(mesh):
    in_specs = (
        P("rep", None, "slab"),
        P("rep", None, "slab"),
        P("slab"),
        P("slab"),
        P("slab"),
        P("rep"),
        P("rep", None, "slab"),
        P("rep", "slab"),
        P("rep", "slab"),
        P(),
    )
    out_specs = (P("rep", None, "slab"), P("rep", None, "slab"), P("rep"))
    return jax.shard_map(local, mesh=mesh, in_specs=in_specs, out_specs=out_specs, check_vma=False)
```

```python
import jax
import jax.numpy as jnp
from jax import lax
from jax.sharding import PartitionSpec as P
from jax.experimental import pallas as pl
from jax.experimental.pallas import tpu as pltpu

CL = 64
CD = 64
STEPS = 4
HALO = 16
NT_MAX = 192
HALF = CL // 2


tile_block = 16
time_step = 0.04
half_step = 0.02
soft_sq = 0.25
slab_width = 2.0
exact = lax.Precision.HIGHEST


def spread_masks():
    rows = lax.broadcasted_iota(jnp.int32, (HALF, CL), 0)
    atoms = lax.broadcasted_iota(jnp.int32, (HALF, CL), 1)
    pick = (atoms // 2 == rows).astype(jnp.float32)
    atoms_t = lax.broadcasted_iota(jnp.int32, (CL, 2 * CL), 0)
    lanes_t = lax.broadcasted_iota(jnp.int32, (CL, 2 * CL), 1)
    place = (atoms_t % 2 == lanes_t // CL).astype(jnp.float32)
    twice = (atoms_t == lanes_t % CL).astype(jnp.float32)
    return pick, place, twice


def split_dot(values, matrix, dims):
    matrix_b = matrix.astype(jnp.bfloat16)
    hi = values.astype(jnp.bfloat16)
    rest = values - hi.astype(jnp.float32)
    mid = rest.astype(jnp.bfloat16)
    lo = (rest - mid.astype(jnp.float32)).astype(jnp.bfloat16)
    total = None
    for part in (hi, mid, lo):
        term = lax.dot_general(part, matrix_b, (dims, ((), ())), preferred_element_type=jnp.float32)
        total = term if total is None else total + term
    return total


def to_columns(values, pick, place):
    width = values.shape[0]
    picked = (values[:, None, :] * pick[None]).reshape(width * HALF, CL)
    spread = split_dot(picked, place, ((1,), (0,)))
    return spread.reshape(width, HALF, 2 * CL)


def from_columns(blocks, pick, place):
    width = blocks.shape[0]
    folded = lax.dot_general(
        blocks.reshape(width * HALF, 2 * CL), place, (((1,), (1,)), ((), ())),
        precision=exact, preferred_element_type=jnp.float32,
    )
    return jnp.sum(folded.reshape(width, HALF, CL) * pick[None], axis=1)


def column_kernel(prm_ref, pcol_ref):
    pick, place, twice = spread_masks()
    owned = pcol_ref.shape[1]
    for c in range(2):
        pcol_ref[c] = to_columns(prm_ref[c, :owned], pick, place)


def param_columns(prm):
    return pl.pallas_call(
        column_kernel,
        out_shape=jax.ShapeDtypeStruct((2, CD, HALF, 2 * CL), jnp.float32),
        compiler_params=pltpu.CompilerParams(vmem_limit_bytes=48 * 1024 * 1024),
    )(prm)


def pair_kernel(tiles_ref, count_ref, ext_ref, prm_ref, pcol_ref, force_ref, en_ref,
                xcol_ref, xrow_ref, prow_ref, fcol_ref, frow_ref):
    pick, place, twice = spread_masks()
    owned = xcol_ref.shape[1]
    for c in range(3):
        xcol_ref[c] = to_columns(ext_ref[c, :owned], pick, place)
        xrow_ref[c] = split_dot(ext_ref[c], twice, ((1,), (0,)))
    for c in range(2):
        prow_ref[c] = split_dot(prm_ref[2 * c], twice, ((1,), (0,)))
    fcol_ref[...] = jnp.zeros(fcol_ref.shape, jnp.float32)
    frow_ref[...] = jnp.zeros(frow_ref.shape, jnp.float32)
    rows = lax.broadcasted_iota(jnp.int32, (HALF, 2 * CL), 0)
    lanes = lax.broadcasted_iota(jnp.int32, (HALF, 2 * CL), 1)
    w_same = jnp.where(2 * rows + lanes // CL == lanes % CL, 0.0, 0.5).astype(jnp.float32)

    def body(t, acc):
        i = tiles_ref[0, t]
        j = tiles_ref[1, t]
        row = pl.ds(j, 1)
        dx = xcol_ref[0, i] - xrow_ref[0, row, :]
        dy = xcol_ref[1, i] - xrow_ref[1, row, :]
        dz = xcol_ref[2, i] - xrow_ref[2, row, :]
        sq = dx * dx + dy * dy + dz * dz
        gauss = pcol_ref[0, i] * prow_ref[0, row, :] * jnp.exp(-sq)
        inv_root = lax.rsqrt(sq + soft_sq)
        coulomb = pcol_ref[1, i] * prow_ref[1, row, :] * inv_root
        same = i == j
        w_force = jnp.where(same, 0.5, 1.0).astype(jnp.float32)
        w_energy = jnp.where(same, w_same, 1.0)
        slope = w_force * (2.0 * gauss + coulomb * inv_root * inv_root)
        px = slope * dx
        py = slope * dy
        pz = slope * dz
        fcol_ref[0, i] += px
        fcol_ref[1, i] += py
        fcol_ref[2, i] += pz
        frow_ref[0, row, :] -= jnp.sum(px, axis=0, keepdims=True)
        frow_ref[1, row, :] -= jnp.sum(py, axis=0, keepdims=True)
        frow_ref[2, row, :] -= jnp.sum(pz, axis=0, keepdims=True)
        return acc + w_energy * (gauss + coulomb)

    acc = lax.fori_loop(0, count_ref[0], body, jnp.zeros((HALF, 2 * CL), jnp.float32))
    en_ref[...] = acc
    for c in range(3):
        f_j = lax.dot_general(
            frow_ref[c], twice, (((1,), (1,)), ((), ())),
            precision=exact, preferred_element_type=jnp.float32,
        )
        force_ref[c, :owned] = from_columns(fcol_ref[c], pick, place) + f_j[:owned]
        force_ref[c, owned:] = f_j[owned:]


def slab_pairs(extended, prm, pcol, tiles, count):
    width = extended.shape[1]
    smem = pl.BlockSpec(memory_space=pltpu.SMEM)
    vmem = pl.BlockSpec(memory_space=pltpu.VMEM)
    forces, acc = pl.pallas_call(
        pair_kernel,
        out_shape=(
            jax.ShapeDtypeStruct((3, width, CL), jnp.float32),
            jax.ShapeDtypeStruct((HALF, 2 * CL), jnp.float32),
        ),
        in_specs=[smem, smem, vmem, vmem, vmem],
        out_specs=(vmem, vmem),
        scratch_shapes=[
            pltpu.VMEM((3, CD, HALF, 2 * CL), jnp.float32),
            pltpu.VMEM((3, width, 2 * CL), jnp.float32),
            pltpu.VMEM((2, width, 2 * CL), jnp.float32),
            pltpu.VMEM((3, CD, HALF, 2 * CL), jnp.float32),
            pltpu.VMEM((3, width, 2 * CL), jnp.float32),
        ],
        compiler_params=pltpu.CompilerParams(vmem_limit_bytes=48 * 1024 * 1024),
    )(tiles, count.reshape(1), extended, prm, pcol)
    return forces, jnp.sum(acc)


def from_behind(value, axis, steps):
    count = lax.axis_size(axis)
    pairs = [(source, (source + steps) % count) for source in range(count)]
    return lax.ppermute(value, axis, pairs)


def partner_of(pair_list, replica_ids):
    first_col = pair_list[:, 0]
    second_col = pair_list[:, 1]
    hit_first = replica_ids[:, None] == first_col[None, :]
    hit_second = replica_ids[:, None] == second_col[None, :]
    partner_sum = jnp.sum(jnp.where(hit_first, second_col[None, :], 0), 1) + jnp.sum(
        jnp.where(hit_second, first_col[None, :], 0), 1
    )
    listed = jnp.any(hit_first, 1) | jnp.any(hit_second, 1)
    return jnp.where(listed, partner_sum, replica_ids)


def exchange(state, swap_pairs):
    count = lax.axis_size("rep")
    rows, width = state.shape
    partner = partner_of(swap_pairs, jnp.arange(count, dtype=jnp.int32))
    chunks = state.reshape(rows, count, width // count).transpose(1, 0, 2)
    spread = lax.all_to_all(chunks, "rep", 0, 0, tiled=True)
    routed = jnp.take(spread, partner, axis=0)
    gathered = lax.all_to_all(routed, "rep", 0, 0, tiled=True)
    return gathered.transpose(1, 0, 2).reshape(rows, width)


def select_table(index_list, width):
    cluster_ids = jnp.arange(width, dtype=jnp.int32)
    return (index_list[:, None] == cluster_ids[None, :]).astype(jnp.float32)


def pair_block(extended, strength_all, charge_all, ham_scale, tile_first, tile_second, live_mask):
    count_tiles = tile_first.shape[0]
    width = extended.shape[1]
    select_first = select_table(tile_first, width)
    select_second = select_table(tile_second, width)
    coords_i = jnp.einsum("te,xec->xct", select_first, extended, precision=exact)
    coords_j = jnp.einsum("te,xec->xtc", select_second, extended, precision=exact)
    offsets = (coords_i[:, :, :, None] - coords_j[:, None, :, :]).reshape(3, CL, count_tiles * CL)
    sq_dist = offsets[0] * offsets[0] + offsets[1] * offsets[1] + offsets[2] * offsets[2]
    params_all = jnp.stack([strength_all, charge_all], 0)
    params_i = jnp.einsum("te,pec->pct", select_first, params_all, precision=exact)
    params_j = jnp.einsum("te,pec->ptc", select_second, params_all, precision=exact)
    strength_prod = (params_i[0][:, :, None] * params_j[0][None, :, :]).reshape(
        CL, count_tiles * CL
    )
    charge_prod = (params_i[1][:, :, None] * params_j[1][None, :, :]).reshape(CL, count_tiles * CL)
    gauss_term = strength_prod * jnp.exp(-sq_dist)
    inv_root = lax.rsqrt(sq_dist + soft_sq)
    coulomb = ham_scale * charge_prod * inv_root
    same_tile = tile_first == tile_second
    weight_tile = jnp.where(live_mask, jnp.where(same_tile, 0.5, 1.0), 0.0).astype(jnp.float32)
    weight_col = jnp.repeat(weight_tile, CL)[None, :]
    slope = gauss_term + 0.5 * coulomb * inv_root * inv_root
    pushes = (2.0 * slope * weight_col)[None, :, :] * offsets
    force_i = pushes.reshape(3, CL, count_tiles, CL).sum(-1)
    force_j = -pushes.sum(1).reshape(3, count_tiles, CL)
    atom_ids = jnp.arange(CL, dtype=jnp.int32)
    column_ids = jnp.arange(count_tiles * CL, dtype=jnp.int32) % CL
    self_pair = jnp.repeat(same_tile, CL)[None, :] & (atom_ids[:, None] == column_ids[None, :])
    energy = jnp.sum(jnp.where(self_pair, 0.0, (gauss_term + coulomb) * weight_col))
    spread_i = jnp.einsum("te,xct->xec", select_first, force_i, precision=exact)
    spread_j = jnp.einsum("te,xtc->xec", select_second, force_j, precision=exact)
    return (spread_i + spread_j, energy)


def local(
    positions,
    velocities,
    inv_mass,
    strength,
    charge,
    scaling,
    tile_pairs,
    tile_counts,
    halo_clusters,
    swap_pairs,
):
    coords = positions[0]
    speeds = velocities[0]
    ham_scale = scaling[0]
    firsts_flat = tile_pairs[0, 0]
    seconds_flat = tile_pairs[0, 1]
    live_count = tile_counts[0, 0]
    halo_index = halo_clusters[0]
    atoms_here = coords.shape[1]
    halo_table = select_table(halo_index, CD)
    params = jnp.stack([strength, charge], 0).reshape(2, CD, CL)
    sent_params = jnp.einsum("hc,pck->phk", halo_table, params, precision=exact).reshape(
        2, HALO * CL
    )
    got_params = from_behind(sent_params, "slab", -1).reshape(2, HALO, CL)
    strength_all = jnp.concatenate([params[0], got_params[0]], 0)
    charge_all = jnp.concatenate([params[1], got_params[1]], 0)
    lift = jnp.array([0.0, 0.0, slab_width], jnp.float32)[:, None]
    param_all = jnp.stack([strength_all, ham_scale * charge_all, charge_all], 0)
    param_cols = param_columns(param_all)
    tile_list = jnp.stack([firsts_flat, seconds_flat], 0)

    def evaluate(coords_now):
        blocks = coords_now.reshape(3, CD, CL)
        sent_coords = jnp.einsum("hc,xck->xhk", halo_table, blocks, precision=exact).reshape(
            3, HALO * CL
        )
        from_above = from_behind(sent_coords, "slab", -1) + lift
        extended = jnp.concatenate([blocks, from_above.reshape(3, HALO, CL)], 1)
        forces, energy = slab_pairs(extended, param_all, param_cols, tile_list, live_count)
        returned = from_behind(forces[:, CD:].reshape(3, HALO * CL), "slab", 1)
        back_home = jnp.einsum(
            "hc,xhk->xck", halo_table, returned.reshape(3, HALO, CL), precision=exact
        )
        local_forces = forces[:, :CD] + back_home
        return (local_forces.reshape(3, atoms_here), energy)

    def verlet_step(step_idx, carry):
        coords, speeds, forces, energy = carry
        speeds = speeds + half_step * forces * inv_mass
        coords = coords + time_step * speeds
        forces, energy = evaluate(coords)
        speeds = speeds + half_step * forces * inv_mass
        return (coords, speeds, forces, energy)

    forces, energy = evaluate(coords)
    coords, speeds, forces, energy = lax.fori_loop(
        0, STEPS, verlet_step, (coords, speeds, forces, energy)
    )
    total_energy = slab_sum(energy)
    potential = (total_energy / (atoms_here * lax.axis_size("slab"))).reshape(1)
    state = jnp.concatenate([coords, speeds], 0)
    swapped = exchange(state, swap_pairs)
    return (swapped[:3][None], swapped[3:][None], potential)


def slab_sum(value):
    count = lax.axis_size("slab")
    stride = 1
    while stride < count:
        pairs = [(source, source ^ stride) for source in range(count)]
        value = value + lax.ppermute(value, "slab", pairs)
        stride *= 2
    return value


def solution(mesh):
    in_specs = (
        P("rep", None, "slab"),
        P("rep", None, "slab"),
        P("slab"),
        P("slab"),
        P("slab"),
        P("rep"),
        P("rep", None, "slab"),
        P("rep", "slab"),
        P("rep", "slab"),
        P(),
    )
    out_specs = (P("rep", None, "slab"), P("rep", None, "slab"), P("rep"))
    return jax.shard_map(local, mesh=mesh, in_specs=in_specs, out_specs=out_specs, check_vma=False)
```

```python
import jax
import jax.numpy as jnp
from jax import lax
from jax.sharding import PartitionSpec as P
from jax.experimental import pallas as pl
from jax.experimental.pallas import tpu as pltpu

CL = 64
CD = 64
STEPS = 4
HALO = 16
NT_MAX = 192
HALF = CL // 2


tile_block = 16
time_step = 0.04
half_step = 0.02
soft_sq = 0.25
slab_width = 2.0
exact = lax.Precision.HIGHEST


def spread_masks():
    rows = lax.broadcasted_iota(jnp.int32, (HALF, CL), 0)
    atoms = lax.broadcasted_iota(jnp.int32, (HALF, CL), 1)
    pick = (atoms // 2 == rows).astype(jnp.float32)
    atoms_t = lax.broadcasted_iota(jnp.int32, (CL, 2 * CL), 0)
    lanes_t = lax.broadcasted_iota(jnp.int32, (CL, 2 * CL), 1)
    place = (atoms_t % 2 == lanes_t // CL).astype(jnp.float32)
    twice = (atoms_t == lanes_t % CL).astype(jnp.float32)
    return pick, place, twice


def split_dot(values, matrix, dims):
    matrix_b = matrix.astype(jnp.bfloat16)
    hi = values.astype(jnp.bfloat16)
    rest = values - hi.astype(jnp.float32)
    mid = rest.astype(jnp.bfloat16)
    lo = (rest - mid.astype(jnp.float32)).astype(jnp.bfloat16)
    total = None
    for part in (hi, mid, lo):
        term = lax.dot_general(part, matrix_b, (dims, ((), ())), preferred_element_type=jnp.float32)
        total = term if total is None else total + term
    return total


def to_columns(values, pick, place):
    width = values.shape[0]
    picked = (values[:, None, :] * pick[None]).reshape(width * HALF, CL)
    spread = split_dot(picked, place, ((1,), (0,)))
    return spread.reshape(width, HALF, 2 * CL)


def from_columns(blocks, pick, place):
    width = blocks.shape[0]
    folded = lax.dot_general(
        blocks.reshape(width * HALF, 2 * CL), place, (((1,), (1,)), ((), ())),
        precision=exact, preferred_element_type=jnp.float32,
    )
    return jnp.sum(folded.reshape(width, HALF, CL) * pick[None], axis=1)


def pair_kernel(tiles_ref, count_ref, ext_ref, prm_ref, force_ref, en_ref,
                xcol_ref, pcol_ref, xrow_ref, prow_ref, fcol_ref, frow_ref):
    pick, place, twice = spread_masks()
    owned = xcol_ref.shape[1]
    for c in range(3):
        xcol_ref[c] = to_columns(ext_ref[c, :owned], pick, place)
        xrow_ref[c] = split_dot(ext_ref[c], twice, ((1,), (0,)))
    for c in range(2):
        pcol_ref[c] = to_columns(prm_ref[c, :owned], pick, place)
        prow_ref[c] = split_dot(prm_ref[2 * c], twice, ((1,), (0,)))
    fcol_ref[...] = jnp.zeros(fcol_ref.shape, jnp.float32)
    frow_ref[...] = jnp.zeros(frow_ref.shape, jnp.float32)
    rows = lax.broadcasted_iota(jnp.int32, (HALF, 2 * CL), 0)
    lanes = lax.broadcasted_iota(jnp.int32, (HALF, 2 * CL), 1)
    w_same = jnp.where(2 * rows + lanes // CL == lanes % CL, 0.0, 0.5).astype(jnp.float32)

    def body(t, acc):
        i = tiles_ref[0, t]
        j = tiles_ref[1, t]
        row = pl.ds(j, 1)
        dx = xcol_ref[0, i] - xrow_ref[0, row, :]
        dy = xcol_ref[1, i] - xrow_ref[1, row, :]
        dz = xcol_ref[2, i] - xrow_ref[2, row, :]
        sq = dx * dx + dy * dy + dz * dz
        gauss = pcol_ref[0, i] * prow_ref[0, row, :] * jnp.exp(-sq)
        inv_root = lax.rsqrt(sq + soft_sq)
        coulomb = pcol_ref[1, i] * prow_ref[1, row, :] * inv_root
        same = i == j
        w_force = jnp.where(same, 0.5, 1.0).astype(jnp.float32)
        w_energy = jnp.where(same, w_same, 1.0)
        slope = w_force * (2.0 * gauss + coulomb * inv_root * inv_root)
        px = slope * dx
        py = slope * dy
        pz = slope * dz
        fcol_ref[0, i] += px
        fcol_ref[1, i] += py
        fcol_ref[2, i] += pz
        frow_ref[0, row, :] -= jnp.sum(px, axis=0, keepdims=True)
        frow_ref[1, row, :] -= jnp.sum(py, axis=0, keepdims=True)
        frow_ref[2, row, :] -= jnp.sum(pz, axis=0, keepdims=True)
        return acc + w_energy * (gauss + coulomb)

    acc = lax.fori_loop(0, count_ref[0], body, jnp.zeros((HALF, 2 * CL), jnp.float32))
    en_ref[...] = acc
    for c in range(3):
        f_j = lax.dot_general(
            frow_ref[c], twice, (((1,), (1,)), ((), ())),
            precision=exact, preferred_element_type=jnp.float32,
        )
        force_ref[c, :owned] = from_columns(fcol_ref[c], pick, place) + f_j[:owned]
        force_ref[c, owned:] = f_j[owned:]


def slab_pairs(extended, prm, tiles, count):
    width = extended.shape[1]
    smem = pl.BlockSpec(memory_space=pltpu.SMEM)
    vmem = pl.BlockSpec(memory_space=pltpu.VMEM)
    forces, acc = pl.pallas_call(
        pair_kernel,
        out_shape=(
            jax.ShapeDtypeStruct((3, width, CL), jnp.float32),
            jax.ShapeDtypeStruct((HALF, 2 * CL), jnp.float32),
        ),
        in_specs=[smem, smem, vmem, vmem],
        out_specs=(vmem, vmem),
        scratch_shapes=[
            pltpu.VMEM((3, CD, HALF, 2 * CL), jnp.float32),
            pltpu.VMEM((2, CD, HALF, 2 * CL), jnp.float32),
            pltpu.VMEM((3, width, 2 * CL), jnp.float32),
            pltpu.VMEM((2, width, 2 * CL), jnp.float32),
            pltpu.VMEM((3, CD, HALF, 2 * CL), jnp.float32),
            pltpu.VMEM((3, width, 2 * CL), jnp.float32),
        ],
        compiler_params=pltpu.CompilerParams(vmem_limit_bytes=48 * 1024 * 1024),
    )(tiles, count.reshape(1), extended, prm)
    return forces, jnp.sum(acc)


def from_behind(value, axis, steps):
    count = lax.axis_size(axis)
    pairs = [(source, (source + steps) % count) for source in range(count)]
    return lax.ppermute(value, axis, pairs)


def partner_of(pair_list, replica_ids):
    first_col = pair_list[:, 0]
    second_col = pair_list[:, 1]
    hit_first = replica_ids[:, None] == first_col[None, :]
    hit_second = replica_ids[:, None] == second_col[None, :]
    partner_sum = jnp.sum(jnp.where(hit_first, second_col[None, :], 0), 1) + jnp.sum(
        jnp.where(hit_second, first_col[None, :], 0), 1
    )
    listed = jnp.any(hit_first, 1) | jnp.any(hit_second, 1)
    return jnp.where(listed, partner_sum, replica_ids)


def exchange(state, swap_pairs):
    count = lax.axis_size("rep")
    rows, width = state.shape
    partner = partner_of(swap_pairs, jnp.arange(count, dtype=jnp.int32))
    chunks = state.reshape(rows, count, width // count).transpose(1, 0, 2)
    spread = lax.all_to_all(chunks, "rep", 0, 0, tiled=True)
    routed = jnp.take(spread, partner, axis=0)
    gathered = lax.all_to_all(routed, "rep", 0, 0, tiled=True)
    return gathered.transpose(1, 0, 2).reshape(rows, width)


def select_table(index_list, width):
    cluster_ids = jnp.arange(width, dtype=jnp.int32)
    return (index_list[:, None] == cluster_ids[None, :]).astype(jnp.float32)


def pair_block(extended, strength_all, charge_all, ham_scale, tile_first, tile_second, live_mask):
    count_tiles = tile_first.shape[0]
    width = extended.shape[1]
    select_first = select_table(tile_first, width)
    select_second = select_table(tile_second, width)
    coords_i = jnp.einsum("te,xec->xct", select_first, extended, precision=exact)
    coords_j = jnp.einsum("te,xec->xtc", select_second, extended, precision=exact)
    offsets = (coords_i[:, :, :, None] - coords_j[:, None, :, :]).reshape(3, CL, count_tiles * CL)
    sq_dist = offsets[0] * offsets[0] + offsets[1] * offsets[1] + offsets[2] * offsets[2]
    params_all = jnp.stack([strength_all, charge_all], 0)
    params_i = jnp.einsum("te,pec->pct", select_first, params_all, precision=exact)
    params_j = jnp.einsum("te,pec->ptc", select_second, params_all, precision=exact)
    strength_prod = (params_i[0][:, :, None] * params_j[0][None, :, :]).reshape(
        CL, count_tiles * CL
    )
    charge_prod = (params_i[1][:, :, None] * params_j[1][None, :, :]).reshape(CL, count_tiles * CL)
    gauss_term = strength_prod * jnp.exp(-sq_dist)
    inv_root = lax.rsqrt(sq_dist + soft_sq)
    coulomb = ham_scale * charge_prod * inv_root
    same_tile = tile_first == tile_second
    weight_tile = jnp.where(live_mask, jnp.where(same_tile, 0.5, 1.0), 0.0).astype(jnp.float32)
    weight_col = jnp.repeat(weight_tile, CL)[None, :]
    slope = gauss_term + 0.5 * coulomb * inv_root * inv_root
    pushes = (2.0 * slope * weight_col)[None, :, :] * offsets
    force_i = pushes.reshape(3, CL, count_tiles, CL).sum(-1)
    force_j = -pushes.sum(1).reshape(3, count_tiles, CL)
    atom_ids = jnp.arange(CL, dtype=jnp.int32)
    column_ids = jnp.arange(count_tiles * CL, dtype=jnp.int32) % CL
    self_pair = jnp.repeat(same_tile, CL)[None, :] & (atom_ids[:, None] == column_ids[None, :])
    energy = jnp.sum(jnp.where(self_pair, 0.0, (gauss_term + coulomb) * weight_col))
    spread_i = jnp.einsum("te,xct->xec", select_first, force_i, precision=exact)
    spread_j = jnp.einsum("te,xtc->xec", select_second, force_j, precision=exact)
    return (spread_i + spread_j, energy)


def local(
    positions,
    velocities,
    inv_mass,
    strength,
    charge,
    scaling,
    tile_pairs,
    tile_counts,
    halo_clusters,
    swap_pairs,
):
    coords = positions[0]
    speeds = velocities[0]
    ham_scale = scaling[0]
    firsts_flat = tile_pairs[0, 0]
    seconds_flat = tile_pairs[0, 1]
    live_count = tile_counts[0, 0]
    halo_index = halo_clusters[0]
    atoms_here = coords.shape[1]
    halo_table = select_table(halo_index, CD)
    params = jnp.stack([strength, charge], 0).reshape(2, CD, CL)
    start_rows = jnp.concatenate([params, coords.reshape(3, CD, CL)], 0)
    sent_start = jnp.einsum("hc,pck->phk", halo_table, start_rows, precision=exact).reshape(
        5, HALO * CL
    )
    got_start = from_behind(sent_start, "slab", -1)
    got_params = got_start[:2].reshape(2, HALO, CL)
    strength_all = jnp.concatenate([params[0], got_params[0]], 0)
    charge_all = jnp.concatenate([params[1], got_params[1]], 0)
    lift = jnp.array([0.0, 0.0, slab_width], jnp.float32)[:, None]
    param_all = jnp.stack([strength_all, ham_scale * charge_all, charge_all], 0)
    tile_list = jnp.stack([firsts_flat, seconds_flat], 0)

    def evaluate(coords_now, received=None):
        blocks = coords_now.reshape(3, CD, CL)
        if received is None:
            sent_coords = jnp.einsum(
                "hc,xck->xhk", halo_table, blocks, precision=exact
            ).reshape(3, HALO * CL)
            received = from_behind(sent_coords, "slab", -1)
        from_above = received + lift
        extended = jnp.concatenate([blocks, from_above.reshape(3, HALO, CL)], 1)
        forces, energy = slab_pairs(extended, param_all, tile_list, live_count)
        returned = from_behind(forces[:, CD:].reshape(3, HALO * CL), "slab", 1)
        back_home = jnp.einsum(
            "hc,xhk->xck", halo_table, returned.reshape(3, HALO, CL), precision=exact
        )
        local_forces = forces[:, :CD] + back_home
        return (local_forces.reshape(3, atoms_here), energy)

    def verlet_step(step_idx, carry):
        coords, speeds, forces, energy = carry
        speeds = speeds + half_step * forces * inv_mass
        coords = coords + time_step * speeds
        forces, energy = evaluate(coords)
        speeds = speeds + half_step * forces * inv_mass
        return (coords, speeds, forces, energy)

    forces, energy = evaluate(coords, got_start[2:])
    coords, speeds, forces, energy = lax.fori_loop(
        0, STEPS, verlet_step, (coords, speeds, forces, energy)
    )
    total_energy = slab_sum(energy)
    potential = (total_energy / (atoms_here * lax.axis_size("slab"))).reshape(1)
    state = jnp.concatenate([coords, speeds], 0)
    swapped = exchange(state, swap_pairs)
    return (swapped[:3][None], swapped[3:][None], potential)


def slab_sum(value):
    count = lax.axis_size("slab")
    stride = 1
    while stride < count:
        pairs = [(source, source ^ stride) for source in range(count)]
        value = value + lax.ppermute(value, "slab", pairs)
        stride *= 2
    return value


def solution(mesh):
    in_specs = (
        P("rep", None, "slab"),
        P("rep", None, "slab"),
        P("slab"),
        P("slab"),
        P("slab"),
        P("rep"),
        P("rep", None, "slab"),
        P("rep", "slab"),
        P("rep", "slab"),
        P(),
    )
    out_specs = (P("rep", None, "slab"), P("rep", None, "slab"), P("rep"))
    return jax.shard_map(local, mesh=mesh, in_specs=in_specs, out_specs=out_specs, check_vma=False)
```

```python
import jax
import jax.numpy as jnp
from jax import lax
from jax.sharding import PartitionSpec as P
from jax.experimental import pallas as pl
from jax.experimental.pallas import tpu as pltpu

CL = 64
CD = 64
STEPS = 4
HALO = 16
NT_MAX = 192
HALF = CL // 2


tile_block = 16
time_step = 0.04
half_step = 0.02
soft_sq = 0.25
slab_width = 2.0
exact = lax.Precision.HIGHEST


def spread_masks():
    rows = lax.broadcasted_iota(jnp.int32, (HALF, CL), 0)
    atoms = lax.broadcasted_iota(jnp.int32, (HALF, CL), 1)
    pick = (atoms // 2 == rows).astype(jnp.float32)
    atoms_t = lax.broadcasted_iota(jnp.int32, (CL, 2 * CL), 0)
    lanes_t = lax.broadcasted_iota(jnp.int32, (CL, 2 * CL), 1)
    place = (atoms_t % 2 == lanes_t // CL).astype(jnp.float32)
    twice = (atoms_t == lanes_t % CL).astype(jnp.float32)
    return pick, place, twice


def split_dot(values, matrix, dims):
    matrix_b = matrix.astype(jnp.bfloat16)
    hi = values.astype(jnp.bfloat16)
    rest = values - hi.astype(jnp.float32)
    mid = rest.astype(jnp.bfloat16)
    lo = (rest - mid.astype(jnp.float32)).astype(jnp.bfloat16)
    total = None
    for part in (hi, mid, lo):
        term = lax.dot_general(part, matrix_b, (dims, ((), ())), preferred_element_type=jnp.float32)
        total = term if total is None else total + term
    return total


def to_columns(values, pick, place):
    width = values.shape[0]
    picked = (values[:, None, :] * pick[None]).reshape(width * HALF, CL)
    spread = split_dot(picked, place, ((1,), (0,)))
    return spread.reshape(width, HALF, 2 * CL)


def from_columns(blocks, pick, place):
    width = blocks.shape[0]
    folded = lax.dot_general(
        blocks.reshape(width * HALF, 2 * CL), place, (((1,), (1,)), ((), ())),
        precision=exact, preferred_element_type=jnp.float32,
    )
    return jnp.sum(folded.reshape(width, HALF, CL) * pick[None], axis=1)


def pair_kernel(tiles_ref, count_ref, ext_ref, prm_ref, force_ref, en_ref,
                xcol_ref, pcol_ref, xrow_ref, prow_ref, fcol_ref, frow_ref):
    pick, place, twice = spread_masks()
    owned = xcol_ref.shape[1]
    for c in range(3):
        xcol_ref[c] = to_columns(ext_ref[c, :owned], pick, place)
        xrow_ref[c] = split_dot(ext_ref[c], twice, ((1,), (0,)))
    for c in range(2):
        pcol_ref[c] = to_columns(prm_ref[c, :owned], pick, place)
        prow_ref[c] = split_dot(prm_ref[2 * c], twice, ((1,), (0,)))
    fcol_ref[...] = jnp.zeros(fcol_ref.shape, jnp.float32)
    frow_ref[...] = jnp.zeros(frow_ref.shape, jnp.float32)
    rows = lax.broadcasted_iota(jnp.int32, (HALF, 2 * CL), 0)
    lanes = lax.broadcasted_iota(jnp.int32, (HALF, 2 * CL), 1)
    w_same = jnp.where(2 * rows + lanes // CL == lanes % CL, 0.0, 0.5).astype(jnp.float32)

    def body(t, acc):
        i = tiles_ref[0, t]
        j = tiles_ref[1, t]
        row = pl.ds(j, 1)
        dx = xcol_ref[0, i] - xrow_ref[0, row, :]
        dy = xcol_ref[1, i] - xrow_ref[1, row, :]
        dz = xcol_ref[2, i] - xrow_ref[2, row, :]
        sq = dx * dx + dy * dy + dz * dz
        gauss = pcol_ref[0, i] * prow_ref[0, row, :] * jnp.exp(-sq)
        inv_root = lax.rsqrt(sq + soft_sq)
        coulomb = pcol_ref[1, i] * prow_ref[1, row, :] * inv_root
        same = i == j
        w_force = jnp.where(same, 0.5, 1.0).astype(jnp.float32)
        w_energy = jnp.where(same, w_same, 1.0)
        slope = w_force * (2.0 * gauss + coulomb * inv_root * inv_root)
        px = slope * dx
        py = slope * dy
        pz = slope * dz
        fcol_ref[0, i] += px
        fcol_ref[1, i] += py
        fcol_ref[2, i] += pz
        frow_ref[0, row, :] -= jnp.sum(px, axis=0, keepdims=True)
        frow_ref[1, row, :] -= jnp.sum(py, axis=0, keepdims=True)
        frow_ref[2, row, :] -= jnp.sum(pz, axis=0, keepdims=True)
        return acc + w_energy * (gauss + coulomb)

    acc = lax.fori_loop(0, count_ref[0], body, jnp.zeros((HALF, 2 * CL), jnp.float32))
    en_ref[...] = acc
    for c in range(3):
        f_j = lax.dot_general(
            frow_ref[c], twice, (((1,), (1,)), ((), ())),
            precision=exact, preferred_element_type=jnp.float32,
        )
        force_ref[c, :owned] = from_columns(fcol_ref[c], pick, place) + f_j[:owned]
        force_ref[c, owned:] = f_j[owned:]


def slab_pairs(extended, prm, tiles, count):
    width = extended.shape[1]
    smem = pl.BlockSpec(memory_space=pltpu.SMEM)
    vmem = pl.BlockSpec(memory_space=pltpu.VMEM)
    forces, acc = pl.pallas_call(
        pair_kernel,
        out_shape=(
            jax.ShapeDtypeStruct((3, width, CL), jnp.float32),
            jax.ShapeDtypeStruct((HALF, 2 * CL), jnp.float32),
        ),
        in_specs=[smem, smem, vmem, vmem],
        out_specs=(vmem, vmem),
        scratch_shapes=[
            pltpu.VMEM((3, CD, HALF, 2 * CL), jnp.float32),
            pltpu.VMEM((2, CD, HALF, 2 * CL), jnp.float32),
            pltpu.VMEM((3, width, 2 * CL), jnp.float32),
            pltpu.VMEM((2, width, 2 * CL), jnp.float32),
            pltpu.VMEM((3, CD, HALF, 2 * CL), jnp.float32),
            pltpu.VMEM((3, width, 2 * CL), jnp.float32),
        ],
        compiler_params=pltpu.CompilerParams(vmem_limit_bytes=48 * 1024 * 1024),
    )(tiles, count.reshape(1), extended, prm)
    return forces, jnp.sum(acc)


def from_behind(value, axis, steps):
    count = lax.axis_size(axis)
    pairs = [(source, (source + steps) % count) for source in range(count)]
    return lax.ppermute(value, axis, pairs)


def partner_of(pair_list, replica_ids):
    first_col = pair_list[:, 0]
    second_col = pair_list[:, 1]
    hit_first = replica_ids[:, None] == first_col[None, :]
    hit_second = replica_ids[:, None] == second_col[None, :]
    partner_sum = jnp.sum(jnp.where(hit_first, second_col[None, :], 0), 1) + jnp.sum(
        jnp.where(hit_second, first_col[None, :], 0), 1
    )
    listed = jnp.any(hit_first, 1) | jnp.any(hit_second, 1)
    return jnp.where(listed, partner_sum, replica_ids)


def exchange(state, swap_pairs):
    count = lax.axis_size("rep")
    rows, width = state.shape
    partner = partner_of(swap_pairs, jnp.arange(count, dtype=jnp.int32))
    chunks = state.reshape(rows, count, width // count).transpose(1, 0, 2)
    spread = lax.all_to_all(chunks, "rep", 0, 0, tiled=True)
    routed = jnp.take(spread, partner, axis=0)
    gathered = lax.all_to_all(routed, "rep", 0, 0, tiled=True)
    return gathered.transpose(1, 0, 2).reshape(rows, width)


def select_table(index_list, width):
    cluster_ids = jnp.arange(width, dtype=jnp.int32)
    return (index_list[:, None] == cluster_ids[None, :]).astype(jnp.float32)


def pair_block(extended, strength_all, charge_all, ham_scale, tile_first, tile_second, live_mask):
    count_tiles = tile_first.shape[0]
    width = extended.shape[1]
    select_first = select_table(tile_first, width)
    select_second = select_table(tile_second, width)
    coords_i = jnp.einsum("te,xec->xct", select_first, extended, precision=exact)
    coords_j = jnp.einsum("te,xec->xtc", select_second, extended, precision=exact)
    offsets = (coords_i[:, :, :, None] - coords_j[:, None, :, :]).reshape(3, CL, count_tiles * CL)
    sq_dist = offsets[0] * offsets[0] + offsets[1] * offsets[1] + offsets[2] * offsets[2]
    params_all = jnp.stack([strength_all, charge_all], 0)
    params_i = jnp.einsum("te,pec->pct", select_first, params_all, precision=exact)
    params_j = jnp.einsum("te,pec->ptc", select_second, params_all, precision=exact)
    strength_prod = (params_i[0][:, :, None] * params_j[0][None, :, :]).reshape(
        CL, count_tiles * CL
    )
    charge_prod = (params_i[1][:, :, None] * params_j[1][None, :, :]).reshape(CL, count_tiles * CL)
    gauss_term = strength_prod * jnp.exp(-sq_dist)
    inv_root = lax.rsqrt(sq_dist + soft_sq)
    coulomb = ham_scale * charge_prod * inv_root
    same_tile = tile_first == tile_second
    weight_tile = jnp.where(live_mask, jnp.where(same_tile, 0.5, 1.0), 0.0).astype(jnp.float32)
    weight_col = jnp.repeat(weight_tile, CL)[None, :]
    slope = gauss_term + 0.5 * coulomb * inv_root * inv_root
    pushes = (2.0 * slope * weight_col)[None, :, :] * offsets
    force_i = pushes.reshape(3, CL, count_tiles, CL).sum(-1)
    force_j = -pushes.sum(1).reshape(3, count_tiles, CL)
    atom_ids = jnp.arange(CL, dtype=jnp.int32)
    column_ids = jnp.arange(count_tiles * CL, dtype=jnp.int32) % CL
    self_pair = jnp.repeat(same_tile, CL)[None, :] & (atom_ids[:, None] == column_ids[None, :])
    energy = jnp.sum(jnp.where(self_pair, 0.0, (gauss_term + coulomb) * weight_col))
    spread_i = jnp.einsum("te,xct->xec", select_first, force_i, precision=exact)
    spread_j = jnp.einsum("te,xtc->xec", select_second, force_j, precision=exact)
    return (spread_i + spread_j, energy)


def local(
    positions,
    velocities,
    inv_mass,
    strength,
    charge,
    scaling,
    tile_pairs,
    tile_counts,
    halo_clusters,
    swap_pairs,
):
    coords = positions[0]
    speeds = velocities[0]
    ham_scale = scaling[0]
    firsts_flat = tile_pairs[0, 0]
    seconds_flat = tile_pairs[0, 1]
    live_count = tile_counts[0, 0]
    halo_index = halo_clusters[0]
    atoms_here = coords.shape[1]
    halo_table = select_table(halo_index, CD)
    params = jnp.stack([strength, charge], 0).reshape(2, CD, CL)
    sent_params = jnp.einsum("hc,pck->phk", halo_table, params, precision=exact).reshape(
        2, HALO * CL
    )
    got_params = from_behind(sent_params, "slab", -1).reshape(2, HALO, CL)
    strength_all = jnp.concatenate([params[0], got_params[0]], 0)
    charge_all = jnp.concatenate([params[1], got_params[1]], 0)
    lift = jnp.array([0.0, 0.0, slab_width], jnp.float32)[:, None]
    param_all = jnp.stack([strength_all, ham_scale * charge_all, charge_all], 0)
    tile_list = jnp.stack([firsts_flat, seconds_flat], 0)

    def evaluate(coords_now):
        blocks = coords_now.reshape(3, CD, CL)
        sent_coords = jnp.einsum("hc,xck->xhk", halo_table, blocks, precision=exact).reshape(
            3, HALO * CL
        )
        from_above = from_behind(sent_coords, "slab", -1) + lift
        extended = jnp.concatenate([blocks, from_above.reshape(3, HALO, CL)], 1)
        forces, energy = slab_pairs(extended, param_all, tile_list, live_count)
        returned = from_behind(forces[:, CD:].reshape(3, HALO * CL), "slab", 1)
        back_home = jnp.einsum(
            "hc,xhk->xck", halo_table, returned.reshape(3, HALO, CL), precision=exact
        )
        local_forces = forces[:, :CD] + back_home
        return (local_forces.reshape(3, atoms_here), energy)

    def verlet_step(step_idx, carry):
        coords, speeds, forces, energy = carry
        speeds = speeds + half_step * forces * inv_mass
        coords = coords + time_step * speeds
        forces, energy = evaluate(coords)
        speeds = speeds + half_step * forces * inv_mass
        return (coords, speeds, forces, energy)

    forces, energy = evaluate(coords)
    coords, speeds, forces, energy = lax.fori_loop(
        0, STEPS, verlet_step, (coords, speeds, forces, energy)
    )
    total_energy = slab_sum(energy)
    potential = (total_energy / (atoms_here * lax.axis_size("slab"))).reshape(1)
    state = jnp.concatenate([coords, speeds], 0) + 0.0 * total_energy
    swapped = exchange(state, swap_pairs)
    return (swapped[:3][None], swapped[3:][None], potential)


def slab_sum(value):
    count = lax.axis_size("slab")
    stride = 1
    while stride < count:
        pairs = [(source, source ^ stride) for source in range(count)]
        value = value + lax.ppermute(value, "slab", pairs)
        stride *= 2
    return value


def solution(mesh):
    in_specs = (
        P("rep", None, "slab"),
        P("rep", None, "slab"),
        P("slab"),
        P("slab"),
        P("slab"),
        P("rep"),
        P("rep", None, "slab"),
        P("rep", "slab"),
        P("rep", "slab"),
        P(),
    )
    out_specs = (P("rep", None, "slab"), P("rep", None, "slab"), P("rep"))
    return jax.shard_map(local, mesh=mesh, in_specs=in_specs, out_specs=out_specs, check_vma=False)
```

```python
import jax
import jax.numpy as jnp
from jax import lax
from jax.sharding import PartitionSpec as P
from jax.experimental import pallas as pl
from jax.experimental.pallas import tpu as pltpu

CL = 64
CD = 64
STEPS = 4
HALO = 16
NT_MAX = 192
HALF = CL // 2


tile_block = 16
time_step = 0.04
half_step = 0.02
soft_sq = 0.25
slab_width = 2.0
exact = lax.Precision.HIGHEST


def spread_masks():
    rows = lax.broadcasted_iota(jnp.int32, (HALF, CL), 0)
    atoms = lax.broadcasted_iota(jnp.int32, (HALF, CL), 1)
    pick = (atoms // 2 == rows).astype(jnp.float32)
    atoms_t = lax.broadcasted_iota(jnp.int32, (CL, 2 * CL), 0)
    lanes_t = lax.broadcasted_iota(jnp.int32, (CL, 2 * CL), 1)
    place = (atoms_t % 2 == lanes_t // CL).astype(jnp.float32)
    twice = (atoms_t == lanes_t % CL).astype(jnp.float32)
    return pick, place, twice


def split_dot(values, matrix, dims):
    matrix_b = matrix.astype(jnp.bfloat16)
    hi = values.astype(jnp.bfloat16)
    rest = values - hi.astype(jnp.float32)
    mid = rest.astype(jnp.bfloat16)
    lo = (rest - mid.astype(jnp.float32)).astype(jnp.bfloat16)
    total = None
    for part in (hi, mid, lo):
        term = lax.dot_general(part, matrix_b, (dims, ((), ())), preferred_element_type=jnp.float32)
        total = term if total is None else total + term
    return total


def to_columns(values, pick, place):
    width = values.shape[0]
    picked = (values[:, None, :] * pick[None]).reshape(width * HALF, CL)
    spread = split_dot(picked, place, ((1,), (0,)))
    return spread.reshape(width, HALF, 2 * CL)


def from_columns(blocks, pick, place):
    width = blocks.shape[0]
    folded = split_dot(blocks.reshape(width * HALF, 2 * CL), place, ((1,), (1,)))
    return jnp.sum(folded.reshape(width, HALF, CL) * pick[None], axis=1)


def pair_kernel(tiles_ref, count_ref, ext_ref, prm_ref, force_ref, en_ref,
                xcol_ref, pcol_ref, xrow_ref, prow_ref, fcol_ref, frow_ref):
    pick, place, twice = spread_masks()
    owned = xcol_ref.shape[1]
    for c in range(3):
        xcol_ref[c] = to_columns(ext_ref[c, :owned], pick, place)
        xrow_ref[c] = split_dot(ext_ref[c], twice, ((1,), (0,)))
    for c in range(2):
        pcol_ref[c] = to_columns(prm_ref[c, :owned], pick, place)
        prow_ref[c] = split_dot(prm_ref[2 * c], twice, ((1,), (0,)))
    fcol_ref[...] = jnp.zeros(fcol_ref.shape, jnp.float32)
    frow_ref[...] = jnp.zeros(frow_ref.shape, jnp.float32)
    rows = lax.broadcasted_iota(jnp.int32, (HALF, 2 * CL), 0)
    lanes = lax.broadcasted_iota(jnp.int32, (HALF, 2 * CL), 1)
    w_same = jnp.where(2 * rows + lanes // CL == lanes % CL, 0.0, 0.5).astype(jnp.float32)

    def body(t, acc):
        i = tiles_ref[0, t]
        j = tiles_ref[1, t]
        row = pl.ds(j, 1)
        dx = xcol_ref[0, i] - xrow_ref[0, row, :]
        dy = xcol_ref[1, i] - xrow_ref[1, row, :]
        dz = xcol_ref[2, i] - xrow_ref[2, row, :]
        sq = dx * dx + dy * dy + dz * dz
        gauss = pcol_ref[0, i] * prow_ref[0, row, :] * jnp.exp(-sq)
        inv_root = lax.rsqrt(sq + soft_sq)
        coulomb = pcol_ref[1, i] * prow_ref[1, row, :] * inv_root
        same = i == j
        w_force = jnp.where(same, 0.5, 1.0).astype(jnp.float32)
        w_energy = jnp.where(same, w_same, 1.0)
        slope = w_force * (2.0 * gauss + coulomb * inv_root * inv_root)
        px = slope * dx
        py = slope * dy
        pz = slope * dz
        fcol_ref[0, i] += px
        fcol_ref[1, i] += py
        fcol_ref[2, i] += pz
        frow_ref[0, row, :] -= jnp.sum(px, axis=0, keepdims=True)
        frow_ref[1, row, :] -= jnp.sum(py, axis=0, keepdims=True)
        frow_ref[2, row, :] -= jnp.sum(pz, axis=0, keepdims=True)
        return acc + w_energy * (gauss + coulomb)

    acc = lax.fori_loop(0, count_ref[0], body, jnp.zeros((HALF, 2 * CL), jnp.float32))
    en_ref[...] = acc
    for c in range(3):
        f_j = lax.dot_general(
            frow_ref[c], twice, (((1,), (1,)), ((), ())),
            precision=exact, preferred_element_type=jnp.float32,
        )
        force_ref[c, :owned] = from_columns(fcol_ref[c], pick, place) + f_j[:owned]
        force_ref[c, owned:] = f_j[owned:]


def slab_pairs(extended, prm, tiles, count):
    width = extended.shape[1]
    smem = pl.BlockSpec(memory_space=pltpu.SMEM)
    vmem = pl.BlockSpec(memory_space=pltpu.VMEM)
    forces, acc = pl.pallas_call(
        pair_kernel,
        out_shape=(
            jax.ShapeDtypeStruct((3, width, CL), jnp.float32),
            jax.ShapeDtypeStruct((HALF, 2 * CL), jnp.float32),
        ),
        in_specs=[smem, smem, vmem, vmem],
        out_specs=(vmem, vmem),
        scratch_shapes=[
            pltpu.VMEM((3, CD, HALF, 2 * CL), jnp.float32),
            pltpu.VMEM((2, CD, HALF, 2 * CL), jnp.float32),
            pltpu.VMEM((3, width, 2 * CL), jnp.float32),
            pltpu.VMEM((2, width, 2 * CL), jnp.float32),
            pltpu.VMEM((3, CD, HALF, 2 * CL), jnp.float32),
            pltpu.VMEM((3, width, 2 * CL), jnp.float32),
        ],
        compiler_params=pltpu.CompilerParams(vmem_limit_bytes=48 * 1024 * 1024),
    )(tiles, count.reshape(1), extended, prm)
    return forces, jnp.sum(acc)


def from_behind(value, axis, steps):
    count = lax.axis_size(axis)
    pairs = [(source, (source + steps) % count) for source in range(count)]
    return lax.ppermute(value, axis, pairs)


def partner_of(pair_list, replica_ids):
    first_col = pair_list[:, 0]
    second_col = pair_list[:, 1]
    hit_first = replica_ids[:, None] == first_col[None, :]
    hit_second = replica_ids[:, None] == second_col[None, :]
    partner_sum = jnp.sum(jnp.where(hit_first, second_col[None, :], 0), 1) + jnp.sum(
        jnp.where(hit_second, first_col[None, :], 0), 1
    )
    listed = jnp.any(hit_first, 1) | jnp.any(hit_second, 1)
    return jnp.where(listed, partner_sum, replica_ids)


def exchange(state, swap_pairs):
    count = lax.axis_size("rep")
    rows, width = state.shape
    partner = partner_of(swap_pairs, jnp.arange(count, dtype=jnp.int32))
    chunks = state.reshape(rows, count, width // count).transpose(1, 0, 2)
    spread = lax.all_to_all(chunks, "rep", 0, 0, tiled=True)
    routed = jnp.take(spread, partner, axis=0)
    gathered = lax.all_to_all(routed, "rep", 0, 0, tiled=True)
    return gathered.transpose(1, 0, 2).reshape(rows, width)


def select_table(index_list, width):
    cluster_ids = jnp.arange(width, dtype=jnp.int32)
    return (index_list[:, None] == cluster_ids[None, :]).astype(jnp.float32)


def pair_block(extended, strength_all, charge_all, ham_scale, tile_first, tile_second, live_mask):
    count_tiles = tile_first.shape[0]
    width = extended.shape[1]
    select_first = select_table(tile_first, width)
    select_second = select_table(tile_second, width)
    coords_i = jnp.einsum("te,xec->xct", select_first, extended, precision=exact)
    coords_j = jnp.einsum("te,xec->xtc", select_second, extended, precision=exact)
    offsets = (coords_i[:, :, :, None] - coords_j[:, None, :, :]).reshape(3, CL, count_tiles * CL)
    sq_dist = offsets[0] * offsets[0] + offsets[1] * offsets[1] + offsets[2] * offsets[2]
    params_all = jnp.stack([strength_all, charge_all], 0)
    params_i = jnp.einsum("te,pec->pct", select_first, params_all, precision=exact)
    params_j = jnp.einsum("te,pec->ptc", select_second, params_all, precision=exact)
    strength_prod = (params_i[0][:, :, None] * params_j[0][None, :, :]).reshape(
        CL, count_tiles * CL
    )
    charge_prod = (params_i[1][:, :, None] * params_j[1][None, :, :]).reshape(CL, count_tiles * CL)
    gauss_term = strength_prod * jnp.exp(-sq_dist)
    inv_root = lax.rsqrt(sq_dist + soft_sq)
    coulomb = ham_scale * charge_prod * inv_root
    same_tile = tile_first == tile_second
    weight_tile = jnp.where(live_mask, jnp.where(same_tile, 0.5, 1.0), 0.0).astype(jnp.float32)
    weight_col = jnp.repeat(weight_tile, CL)[None, :]
    slope = gauss_term + 0.5 * coulomb * inv_root * inv_root
    pushes = (2.0 * slope * weight_col)[None, :, :] * offsets
    force_i = pushes.reshape(3, CL, count_tiles, CL).sum(-1)
    force_j = -pushes.sum(1).reshape(3, count_tiles, CL)
    atom_ids = jnp.arange(CL, dtype=jnp.int32)
    column_ids = jnp.arange(count_tiles * CL, dtype=jnp.int32) % CL
    self_pair = jnp.repeat(same_tile, CL)[None, :] & (atom_ids[:, None] == column_ids[None, :])
    energy = jnp.sum(jnp.where(self_pair, 0.0, (gauss_term + coulomb) * weight_col))
    spread_i = jnp.einsum("te,xct->xec", select_first, force_i, precision=exact)
    spread_j = jnp.einsum("te,xtc->xec", select_second, force_j, precision=exact)
    return (spread_i + spread_j, energy)


def local(
    positions,
    velocities,
    inv_mass,
    strength,
    charge,
    scaling,
    tile_pairs,
    tile_counts,
    halo_clusters,
    swap_pairs,
):
    coords = positions[0]
    speeds = velocities[0]
    ham_scale = scaling[0]
    firsts_flat = tile_pairs[0, 0]
    seconds_flat = tile_pairs[0, 1]
    live_count = tile_counts[0, 0]
    halo_index = halo_clusters[0]
    atoms_here = coords.shape[1]
    halo_table = select_table(halo_index, CD)
    params = jnp.stack([strength, charge], 0).reshape(2, CD, CL)
    sent_params = jnp.einsum("hc,pck->phk", halo_table, params, precision=exact).reshape(
        2, HALO * CL
    )
    got_params = from_behind(sent_params, "slab", -1).reshape(2, HALO, CL)
    strength_all = jnp.concatenate([params[0], got_params[0]], 0)
    charge_all = jnp.concatenate([params[1], got_params[1]], 0)
    lift = jnp.array([0.0, 0.0, slab_width], jnp.float32)[:, None]
    param_all = jnp.stack([strength_all, ham_scale * charge_all, charge_all], 0)
    tile_list = jnp.stack([firsts_flat, seconds_flat], 0)

    def evaluate(coords_now):
        blocks = coords_now.reshape(3, CD, CL)
        sent_coords = jnp.einsum("hc,xck->xhk", halo_table, blocks, precision=exact).reshape(
            3, HALO * CL
        )
        from_above = from_behind(sent_coords, "slab", -1) + lift
        extended = jnp.concatenate([blocks, from_above.reshape(3, HALO, CL)], 1)
        forces, energy = slab_pairs(extended, param_all, tile_list, live_count)
        returned = from_behind(forces[:, CD:].reshape(3, HALO * CL), "slab", 1)
        back_home = jnp.einsum(
            "hc,xhk->xck", halo_table, returned.reshape(3, HALO, CL), precision=exact
        )
        local_forces = forces[:, :CD] + back_home
        return (local_forces.reshape(3, atoms_here), energy)

    def verlet_step(step_idx, carry):
        coords, speeds, forces, energy = carry
        speeds = speeds + half_step * forces * inv_mass
        coords = coords + time_step * speeds
        forces, energy = evaluate(coords)
        speeds = speeds + half_step * forces * inv_mass
        return (coords, speeds, forces, energy)

    forces, energy = evaluate(coords)
    coords, speeds, forces, energy = lax.fori_loop(
        0, STEPS, verlet_step, (coords, speeds, forces, energy)
    )
    total_energy = slab_sum(energy)
    potential = (total_energy / (atoms_here * lax.axis_size("slab"))).reshape(1)
    state = jnp.concatenate([coords, speeds], 0)
    swapped = exchange(state, swap_pairs)
    return (swapped[:3][None], swapped[3:][None], potential)


def slab_sum(value):
    count = lax.axis_size("slab")
    stride = 1
    while stride < count:
        pairs = [(source, source ^ stride) for source in range(count)]
        value = value + lax.ppermute(value, "slab", pairs)
        stride *= 2
    return value


def solution(mesh):
    in_specs = (
        P("rep", None, "slab"),
        P("rep", None, "slab"),
        P("slab"),
        P("slab"),
        P("slab"),
        P("rep"),
        P("rep", None, "slab"),
        P("rep", "slab"),
        P("rep", "slab"),
        P(),
    )
    out_specs = (P("rep", None, "slab"), P("rep", None, "slab"), P("rep"))
    return jax.shard_map(local, mesh=mesh, in_specs=in_specs, out_specs=out_specs, check_vma=False)
```

```python
import jax
import jax.numpy as jnp
from jax import lax
from jax.sharding import PartitionSpec as P
from jax.experimental import pallas as pl
from jax.experimental.pallas import tpu as pltpu

CL = 64
CD = 64
STEPS = 4
HALO = 16
NT_MAX = 192
HALF = CL // 2


tile_block = 16
time_step = 0.04
half_step = 0.02
soft_sq = 0.25
slab_width = 2.0
exact = lax.Precision.HIGHEST


def spread_masks():
    rows = lax.broadcasted_iota(jnp.int32, (HALF, CL), 0)
    atoms = lax.broadcasted_iota(jnp.int32, (HALF, CL), 1)
    pick = (atoms // 2 == rows).astype(jnp.float32)
    atoms_t = lax.broadcasted_iota(jnp.int32, (CL, 2 * CL), 0)
    lanes_t = lax.broadcasted_iota(jnp.int32, (CL, 2 * CL), 1)
    place = (atoms_t % 2 == lanes_t // CL).astype(jnp.float32)
    twice = (atoms_t == lanes_t % CL).astype(jnp.float32)
    return pick, place, twice


def split_dot(values, matrix, dims):
    matrix_b = matrix.astype(jnp.bfloat16)
    hi = values.astype(jnp.bfloat16)
    rest = values - hi.astype(jnp.float32)
    mid = rest.astype(jnp.bfloat16)
    lo = (rest - mid.astype(jnp.float32)).astype(jnp.bfloat16)
    total = None
    for part in (hi, mid, lo):
        term = lax.dot_general(part, matrix_b, (dims, ((), ())), preferred_element_type=jnp.float32)
        total = term if total is None else total + term
    return total


def to_columns(values, pick, place):
    width = values.shape[0]
    picked = (values[:, None, :] * pick[None]).reshape(width * HALF, CL)
    spread = split_dot(picked, place, ((1,), (0,)))
    return spread.reshape(width, HALF, 2 * CL)


def from_columns(blocks, pick, place):
    width = blocks.shape[0]
    folded = split_dot(blocks.reshape(width * HALF, 2 * CL), place, ((1,), (1,)))
    return jnp.sum(folded.reshape(width, HALF, CL) * pick[None], axis=1)


def pair_kernel(tiles_ref, count_ref, ext_ref, prm_ref, force_ref, en_ref,
                xcol_ref, pcol_ref, xrow_ref, prow_ref, fcol_ref, frow_ref):
    pick, place, twice = spread_masks()
    owned = xcol_ref.shape[1]
    for c in range(3):
        xcol_ref[c] = to_columns(ext_ref[c, :owned], pick, place)
        xrow_ref[c] = split_dot(ext_ref[c], twice, ((1,), (0,)))
    for c in range(2):
        pcol_ref[c] = to_columns(prm_ref[c, :owned], pick, place)
        prow_ref[c] = split_dot(prm_ref[2 * c], twice, ((1,), (0,)))
    fcol_ref[...] = jnp.zeros(fcol_ref.shape, jnp.float32)
    frow_ref[...] = jnp.zeros(frow_ref.shape, jnp.float32)
    rows = lax.broadcasted_iota(jnp.int32, (HALF, 2 * CL), 0)
    lanes = lax.broadcasted_iota(jnp.int32, (HALF, 2 * CL), 1)
    w_same = jnp.where(2 * rows + lanes // CL == lanes % CL, 0.0, 0.5).astype(jnp.float32)

    def body(t, acc):
        i = tiles_ref[0, t]
        j = tiles_ref[1, t]
        row = pl.ds(j, 1)
        dx = xcol_ref[0, i] - xrow_ref[0, row, :]
        dy = xcol_ref[1, i] - xrow_ref[1, row, :]
        dz = xcol_ref[2, i] - xrow_ref[2, row, :]
        sq = dx * dx + dy * dy + dz * dz
        gauss = pcol_ref[0, i] * prow_ref[0, row, :] * jnp.exp(-sq)
        inv_root = lax.rsqrt(sq + soft_sq)
        coulomb = pcol_ref[1, i] * prow_ref[1, row, :] * inv_root
        same = i == j
        w_force = jnp.where(same, 0.5, 1.0).astype(jnp.float32)
        w_energy = jnp.where(same, w_same, 1.0)
        slope = w_force * (2.0 * gauss + coulomb * inv_root * inv_root)
        px = slope * dx
        py = slope * dy
        pz = slope * dz
        fcol_ref[0, i] += px
        fcol_ref[1, i] += py
        fcol_ref[2, i] += pz
        frow_ref[0, row, :] -= jnp.sum(px, axis=0, keepdims=True)
        frow_ref[1, row, :] -= jnp.sum(py, axis=0, keepdims=True)
        frow_ref[2, row, :] -= jnp.sum(pz, axis=0, keepdims=True)
        return acc + w_energy * (gauss + coulomb)

    acc = lax.fori_loop(0, count_ref[0], body, jnp.zeros((HALF, 2 * CL), jnp.float32))
    en_ref[...] = acc
    for c in range(3):
        f_j = split_dot(frow_ref[c], twice, ((1,), (1,)))
        force_ref[c, :owned] = from_columns(fcol_ref[c], pick, place) + f_j[:owned]
        force_ref[c, owned:] = f_j[owned:]


def slab_pairs(extended, prm, tiles, count):
    width = extended.shape[1]
    smem = pl.BlockSpec(memory_space=pltpu.SMEM)
    vmem = pl.BlockSpec(memory_space=pltpu.VMEM)
    forces, acc = pl.pallas_call(
        pair_kernel,
        out_shape=(
            jax.ShapeDtypeStruct((3, width, CL), jnp.float32),
            jax.ShapeDtypeStruct((HALF, 2 * CL), jnp.float32),
        ),
        in_specs=[smem, smem, vmem, vmem],
        out_specs=(vmem, vmem),
        scratch_shapes=[
            pltpu.VMEM((3, CD, HALF, 2 * CL), jnp.float32),
            pltpu.VMEM((2, CD, HALF, 2 * CL), jnp.float32),
            pltpu.VMEM((3, width, 2 * CL), jnp.float32),
            pltpu.VMEM((2, width, 2 * CL), jnp.float32),
            pltpu.VMEM((3, CD, HALF, 2 * CL), jnp.float32),
            pltpu.VMEM((3, width, 2 * CL), jnp.float32),
        ],
        compiler_params=pltpu.CompilerParams(vmem_limit_bytes=48 * 1024 * 1024),
    )(tiles, count.reshape(1), extended, prm)
    return forces, jnp.sum(acc)


def from_behind(value, axis, steps):
    count = lax.axis_size(axis)
    pairs = [(source, (source + steps) % count) for source in range(count)]
    return lax.ppermute(value, axis, pairs)


def partner_of(pair_list, replica_ids):
    first_col = pair_list[:, 0]
    second_col = pair_list[:, 1]
    hit_first = replica_ids[:, None] == first_col[None, :]
    hit_second = replica_ids[:, None] == second_col[None, :]
    partner_sum = jnp.sum(jnp.where(hit_first, second_col[None, :], 0), 1) + jnp.sum(
        jnp.where(hit_second, first_col[None, :], 0), 1
    )
    listed = jnp.any(hit_first, 1) | jnp.any(hit_second, 1)
    return jnp.where(listed, partner_sum, replica_ids)


def exchange(state, swap_pairs):
    count = lax.axis_size("rep")
    rows, width = state.shape
    partner = partner_of(swap_pairs, jnp.arange(count, dtype=jnp.int32))
    chunks = state.reshape(rows, count, width // count).transpose(1, 0, 2)
    spread = lax.all_to_all(chunks, "rep", 0, 0, tiled=True)
    routed = jnp.take(spread, partner, axis=0)
    gathered = lax.all_to_all(routed, "rep", 0, 0, tiled=True)
    return gathered.transpose(1, 0, 2).reshape(rows, width)


def select_table(index_list, width):
    cluster_ids = jnp.arange(width, dtype=jnp.int32)
    return (index_list[:, None] == cluster_ids[None, :]).astype(jnp.float32)


def pair_block(extended, strength_all, charge_all, ham_scale, tile_first, tile_second, live_mask):
    count_tiles = tile_first.shape[0]
    width = extended.shape[1]
    select_first = select_table(tile_first, width)
    select_second = select_table(tile_second, width)
    coords_i = jnp.einsum("te,xec->xct", select_first, extended, precision=exact)
    coords_j = jnp.einsum("te,xec->xtc", select_second, extended, precision=exact)
    offsets = (coords_i[:, :, :, None] - coords_j[:, None, :, :]).reshape(3, CL, count_tiles * CL)
    sq_dist = offsets[0] * offsets[0] + offsets[1] * offsets[1] + offsets[2] * offsets[2]
    params_all = jnp.stack([strength_all, charge_all], 0)
    params_i = jnp.einsum("te,pec->pct", select_first, params_all, precision=exact)
    params_j = jnp.einsum("te,pec->ptc", select_second, params_all, precision=exact)
    strength_prod = (params_i[0][:, :, None] * params_j[0][None, :, :]).reshape(
        CL, count_tiles * CL
    )
    charge_prod = (params_i[1][:, :, None] * params_j[1][None, :, :]).reshape(CL, count_tiles * CL)
    gauss_term = strength_prod * jnp.exp(-sq_dist)
    inv_root = lax.rsqrt(sq_dist + soft_sq)
    coulomb = ham_scale * charge_prod * inv_root
    same_tile = tile_first == tile_second
    weight_tile = jnp.where(live_mask, jnp.where(same_tile, 0.5, 1.0), 0.0).astype(jnp.float32)
    weight_col = jnp.repeat(weight_tile, CL)[None, :]
    slope = gauss_term + 0.5 * coulomb * inv_root * inv_root
    pushes = (2.0 * slope * weight_col)[None, :, :] * offsets
    force_i = pushes.reshape(3, CL, count_tiles, CL).sum(-1)
    force_j = -pushes.sum(1).reshape(3, count_tiles, CL)
    atom_ids = jnp.arange(CL, dtype=jnp.int32)
    column_ids = jnp.arange(count_tiles * CL, dtype=jnp.int32) % CL
    self_pair = jnp.repeat(same_tile, CL)[None, :] & (atom_ids[:, None] == column_ids[None, :])
    energy = jnp.sum(jnp.where(self_pair, 0.0, (gauss_term + coulomb) * weight_col))
    spread_i = jnp.einsum("te,xct->xec", select_first, force_i, precision=exact)
    spread_j = jnp.einsum("te,xtc->xec", select_second, force_j, precision=exact)
    return (spread_i + spread_j, energy)


def local(
    positions,
    velocities,
    inv_mass,
    strength,
    charge,
    scaling,
    tile_pairs,
    tile_counts,
    halo_clusters,
    swap_pairs,
):
    coords = positions[0]
    speeds = velocities[0]
    ham_scale = scaling[0]
    firsts_flat = tile_pairs[0, 0]
    seconds_flat = tile_pairs[0, 1]
    live_count = tile_counts[0, 0]
    halo_index = halo_clusters[0]
    atoms_here = coords.shape[1]
    halo_table = select_table(halo_index, CD)
    params = jnp.stack([strength, charge], 0).reshape(2, CD, CL)
    sent_params = jnp.einsum("hc,pck->phk", halo_table, params, precision=exact).reshape(
        2, HALO * CL
    )
    got_params = from_behind(sent_params, "slab", -1).reshape(2, HALO, CL)
    strength_all = jnp.concatenate([params[0], got_params[0]], 0)
    charge_all = jnp.concatenate([params[1], got_params[1]], 0)
    lift = jnp.array([0.0, 0.0, slab_width], jnp.float32)[:, None]
    param_all = jnp.stack([strength_all, ham_scale * charge_all, charge_all], 0)
    tile_list = jnp.stack([firsts_flat, seconds_flat], 0)

    def evaluate(coords_now):
        blocks = coords_now.reshape(3, CD, CL)
        sent_coords = jnp.einsum("hc,xck->xhk", halo_table, blocks, precision=exact).reshape(
            3, HALO * CL
        )
        from_above = from_behind(sent_coords, "slab", -1) + lift
        extended = jnp.concatenate([blocks, from_above.reshape(3, HALO, CL)], 1)
        forces, energy = slab_pairs(extended, param_all, tile_list, live_count)
        returned = from_behind(forces[:, CD:].reshape(3, HALO * CL), "slab", 1)
        back_home = jnp.einsum(
            "hc,xhk->xck", halo_table, returned.reshape(3, HALO, CL), precision=exact
        )
        local_forces = forces[:, :CD] + back_home
        return (local_forces.reshape(3, atoms_here), energy)

    def verlet_step(step_idx, carry):
        coords, speeds, forces, energy = carry
        speeds = speeds + half_step * forces * inv_mass
        coords = coords + time_step * speeds
        forces, energy = evaluate(coords)
        speeds = speeds + half_step * forces * inv_mass
        return (coords, speeds, forces, energy)

    forces, energy = evaluate(coords)
    coords, speeds, forces, energy = lax.fori_loop(
        0, STEPS, verlet_step, (coords, speeds, forces, energy)
    )
    total_energy = slab_sum(energy)
    potential = (total_energy / (atoms_here * lax.axis_size("slab"))).reshape(1)
    state = jnp.concatenate([coords, speeds], 0)
    swapped = exchange(state, swap_pairs)
    return (swapped[:3][None], swapped[3:][None], potential)


def slab_sum(value):
    count = lax.axis_size("slab")
    stride = 1
    while stride < count:
        pairs = [(source, source ^ stride) for source in range(count)]
        value = value + lax.ppermute(value, "slab", pairs)
        stride *= 2
    return value


def solution(mesh):
    in_specs = (
        P("rep", None, "slab"),
        P("rep", None, "slab"),
        P("slab"),
        P("slab"),
        P("slab"),
        P("rep"),
        P("rep", None, "slab"),
        P("rep", "slab"),
        P("rep", "slab"),
        P(),
    )
    out_specs = (P("rep", None, "slab"), P("rep", None, "slab"), P("rep"))
    return jax.shard_map(local, mesh=mesh, in_specs=in_specs, out_specs=out_specs, check_vma=False)
```

```python
import jax
import jax.numpy as jnp
from jax import lax
from jax.sharding import PartitionSpec as P
from jax.experimental import pallas as pl
from jax.experimental.pallas import tpu as pltpu

CL = 64
CD = 64
STEPS = 4
HALO = 16
NT_MAX = 192
HALF = CL // 2


tile_block = 16
time_step = 0.04
half_step = 0.02
soft_sq = 0.25
slab_width = 2.0
exact = lax.Precision.HIGHEST


def spread_masks():
    rows = lax.broadcasted_iota(jnp.int32, (HALF, CL), 0)
    atoms = lax.broadcasted_iota(jnp.int32, (HALF, CL), 1)
    pick = (atoms // 2 == rows).astype(jnp.float32)
    atoms_t = lax.broadcasted_iota(jnp.int32, (CL, 2 * CL), 0)
    lanes_t = lax.broadcasted_iota(jnp.int32, (CL, 2 * CL), 1)
    place = (atoms_t % 2 == lanes_t // CL).astype(jnp.float32)
    twice = (atoms_t == lanes_t % CL).astype(jnp.float32)
    return pick, place, twice


def split_dot(values, matrix, dims):
    matrix_b = matrix.astype(jnp.bfloat16)
    hi = values.astype(jnp.bfloat16)
    rest = values - hi.astype(jnp.float32)
    mid = rest.astype(jnp.bfloat16)
    lo = (rest - mid.astype(jnp.float32)).astype(jnp.bfloat16)
    total = None
    for part in (hi, mid, lo):
        term = lax.dot_general(part, matrix_b, (dims, ((), ())), preferred_element_type=jnp.float32)
        total = term if total is None else total + term
    return total


def to_columns(values, pick, place):
    width = values.shape[0]
    place_b = place.astype(jnp.bfloat16)
    hi = values.astype(jnp.bfloat16)
    rest = values - hi.astype(jnp.float32)
    mid = rest.astype(jnp.bfloat16)
    lo = (rest - mid.astype(jnp.float32)).astype(jnp.bfloat16)
    chosen = pick[None] > 0.0
    spread = None
    for part in (hi, mid, lo):
        picked = jnp.where(chosen, part[:, None, :], jnp.zeros((), jnp.bfloat16))
        term = jnp.dot(picked.reshape(width * HALF, CL), place_b, preferred_element_type=jnp.float32)
        spread = term if spread is None else spread + term
    return spread.reshape(width, HALF, 2 * CL)


def from_columns(blocks, pick, place):
    width = blocks.shape[0]
    folded = split_dot(blocks.reshape(width * HALF, 2 * CL), place, ((1,), (1,)))
    return jnp.sum(folded.reshape(width, HALF, CL) * pick[None], axis=1)


def pair_kernel(tiles_ref, count_ref, ext_ref, prm_ref, force_ref, en_ref,
                xcol_ref, pcol_ref, xrow_ref, prow_ref, fcol_ref, frow_ref):
    pick, place, twice = spread_masks()
    owned = xcol_ref.shape[1]
    for c in range(3):
        xcol_ref[c] = to_columns(ext_ref[c, :owned], pick, place)
        xrow_ref[c] = split_dot(ext_ref[c], twice, ((1,), (0,)))
    for c in range(2):
        pcol_ref[c] = to_columns(prm_ref[c, :owned], pick, place)
        prow_ref[c] = split_dot(prm_ref[2 * c], twice, ((1,), (0,)))
    fcol_ref[...] = jnp.zeros(fcol_ref.shape, jnp.float32)
    frow_ref[...] = jnp.zeros(frow_ref.shape, jnp.float32)
    rows = lax.broadcasted_iota(jnp.int32, (HALF, 2 * CL), 0)
    lanes = lax.broadcasted_iota(jnp.int32, (HALF, 2 * CL), 1)
    w_same = jnp.where(2 * rows + lanes // CL == lanes % CL, 0.0, 0.5).astype(jnp.float32)

    def body(t, acc):
        i = tiles_ref[0, t]
        j = tiles_ref[1, t]
        row = pl.ds(j, 1)
        dx = xcol_ref[0, i] - xrow_ref[0, row, :]
        dy = xcol_ref[1, i] - xrow_ref[1, row, :]
        dz = xcol_ref[2, i] - xrow_ref[2, row, :]
        sq = dx * dx + dy * dy + dz * dz
        gauss = pcol_ref[0, i] * prow_ref[0, row, :] * jnp.exp(-sq)
        inv_root = lax.rsqrt(sq + soft_sq)
        coulomb = pcol_ref[1, i] * prow_ref[1, row, :] * inv_root
        same = i == j
        w_force = jnp.where(same, 0.5, 1.0).astype(jnp.float32)
        w_energy = jnp.where(same, w_same, 1.0)
        slope = w_force * (2.0 * gauss + coulomb * inv_root * inv_root)
        px = slope * dx
        py = slope * dy
        pz = slope * dz
        fcol_ref[0, i] += px
        fcol_ref[1, i] += py
        fcol_ref[2, i] += pz
        frow_ref[0, row, :] -= jnp.sum(px, axis=0, keepdims=True)
        frow_ref[1, row, :] -= jnp.sum(py, axis=0, keepdims=True)
        frow_ref[2, row, :] -= jnp.sum(pz, axis=0, keepdims=True)
        return acc + w_energy * (gauss + coulomb)

    acc = lax.fori_loop(0, count_ref[0], body, jnp.zeros((HALF, 2 * CL), jnp.float32))
    en_ref[...] = acc
    for c in range(3):
        f_j = lax.dot_general(
            frow_ref[c], twice, (((1,), (1,)), ((), ())),
            precision=exact, preferred_element_type=jnp.float32,
        )
        force_ref[c, :owned] = from_columns(fcol_ref[c], pick, place) + f_j[:owned]
        force_ref[c, owned:] = f_j[owned:]


def slab_pairs(extended, prm, tiles, count):
    width = extended.shape[1]
    smem = pl.BlockSpec(memory_space=pltpu.SMEM)
    vmem = pl.BlockSpec(memory_space=pltpu.VMEM)
    forces, acc = pl.pallas_call(
        pair_kernel,
        out_shape=(
            jax.ShapeDtypeStruct((3, width, CL), jnp.float32),
            jax.ShapeDtypeStruct((HALF, 2 * CL), jnp.float32),
        ),
        in_specs=[smem, smem, vmem, vmem],
        out_specs=(vmem, vmem),
        scratch_shapes=[
            pltpu.VMEM((3, CD, HALF, 2 * CL), jnp.float32),
            pltpu.VMEM((2, CD, HALF, 2 * CL), jnp.float32),
            pltpu.VMEM((3, width, 2 * CL), jnp.float32),
            pltpu.VMEM((2, width, 2 * CL), jnp.float32),
            pltpu.VMEM((3, CD, HALF, 2 * CL), jnp.float32),
            pltpu.VMEM((3, width, 2 * CL), jnp.float32),
        ],
        compiler_params=pltpu.CompilerParams(vmem_limit_bytes=48 * 1024 * 1024),
    )(tiles, count.reshape(1), extended, prm)
    return forces, jnp.sum(acc)


def from_behind(value, axis, steps):
    count = lax.axis_size(axis)
    pairs = [(source, (source + steps) % count) for source in range(count)]
    return lax.ppermute(value, axis, pairs)


def partner_of(pair_list, replica_ids):
    first_col = pair_list[:, 0]
    second_col = pair_list[:, 1]
    hit_first = replica_ids[:, None] == first_col[None, :]
    hit_second = replica_ids[:, None] == second_col[None, :]
    partner_sum = jnp.sum(jnp.where(hit_first, second_col[None, :], 0), 1) + jnp.sum(
        jnp.where(hit_second, first_col[None, :], 0), 1
    )
    listed = jnp.any(hit_first, 1) | jnp.any(hit_second, 1)
    return jnp.where(listed, partner_sum, replica_ids)


def exchange(state, swap_pairs):
    count = lax.axis_size("rep")
    rows, width = state.shape
    partner = partner_of(swap_pairs, jnp.arange(count, dtype=jnp.int32))
    chunks = state.reshape(rows, count, width // count).transpose(1, 0, 2)
    spread = lax.all_to_all(chunks, "rep", 0, 0, tiled=True)
    routed = jnp.take(spread, partner, axis=0)
    gathered = lax.all_to_all(routed, "rep", 0, 0, tiled=True)
    return gathered.transpose(1, 0, 2).reshape(rows, width)


def select_table(index_list, width):
    cluster_ids = jnp.arange(width, dtype=jnp.int32)
    return (index_list[:, None] == cluster_ids[None, :]).astype(jnp.float32)


def pair_block(extended, strength_all, charge_all, ham_scale, tile_first, tile_second, live_mask):
    count_tiles = tile_first.shape[0]
    width = extended.shape[1]
    select_first = select_table(tile_first, width)
    select_second = select_table(tile_second, width)
    coords_i = jnp.einsum("te,xec->xct", select_first, extended, precision=exact)
    coords_j = jnp.einsum("te,xec->xtc", select_second, extended, precision=exact)
    offsets = (coords_i[:, :, :, None] - coords_j[:, None, :, :]).reshape(3, CL, count_tiles * CL)
    sq_dist = offsets[0] * offsets[0] + offsets[1] * offsets[1] + offsets[2] * offsets[2]
    params_all = jnp.stack([strength_all, charge_all], 0)
    params_i = jnp.einsum("te,pec->pct", select_first, params_all, precision=exact)
    params_j = jnp.einsum("te,pec->ptc", select_second, params_all, precision=exact)
    strength_prod = (params_i[0][:, :, None] * params_j[0][None, :, :]).reshape(
        CL, count_tiles * CL
    )
    charge_prod = (params_i[1][:, :, None] * params_j[1][None, :, :]).reshape(CL, count_tiles * CL)
    gauss_term = strength_prod * jnp.exp(-sq_dist)
    inv_root = lax.rsqrt(sq_dist + soft_sq)
    coulomb = ham_scale * charge_prod * inv_root
    same_tile = tile_first == tile_second
    weight_tile = jnp.where(live_mask, jnp.where(same_tile, 0.5, 1.0), 0.0).astype(jnp.float32)
    weight_col = jnp.repeat(weight_tile, CL)[None, :]
    slope = gauss_term + 0.5 * coulomb * inv_root * inv_root
    pushes = (2.0 * slope * weight_col)[None, :, :] * offsets
    force_i = pushes.reshape(3, CL, count_tiles, CL).sum(-1)
    force_j = -pushes.sum(1).reshape(3, count_tiles, CL)
    atom_ids = jnp.arange(CL, dtype=jnp.int32)
    column_ids = jnp.arange(count_tiles * CL, dtype=jnp.int32) % CL
    self_pair = jnp.repeat(same_tile, CL)[None, :] & (atom_ids[:, None] == column_ids[None, :])
    energy = jnp.sum(jnp.where(self_pair, 0.0, (gauss_term + coulomb) * weight_col))
    spread_i = jnp.einsum("te,xct->xec", select_first, force_i, precision=exact)
    spread_j = jnp.einsum("te,xtc->xec", select_second, force_j, precision=exact)
    return (spread_i + spread_j, energy)


def local(
    positions,
    velocities,
    inv_mass,
    strength,
    charge,
    scaling,
    tile_pairs,
    tile_counts,
    halo_clusters,
    swap_pairs,
):
    coords = positions[0]
    speeds = velocities[0]
    ham_scale = scaling[0]
    firsts_flat = tile_pairs[0, 0]
    seconds_flat = tile_pairs[0, 1]
    live_count = tile_counts[0, 0]
    halo_index = halo_clusters[0]
    atoms_here = coords.shape[1]
    halo_table = select_table(halo_index, CD)
    params = jnp.stack([strength, charge], 0).reshape(2, CD, CL)
    sent_params = jnp.einsum("hc,pck->phk", halo_table, params, precision=exact).reshape(
        2, HALO * CL
    )
    got_params = from_behind(sent_params, "slab", -1).reshape(2, HALO, CL)
    strength_all = jnp.concatenate([params[0], got_params[0]], 0)
    charge_all = jnp.concatenate([params[1], got_params[1]], 0)
    lift = jnp.array([0.0, 0.0, slab_width], jnp.float32)[:, None]
    param_all = jnp.stack([strength_all, ham_scale * charge_all, charge_all], 0)
    tile_list = jnp.stack([firsts_flat, seconds_flat], 0)

    def evaluate(coords_now):
        blocks = coords_now.reshape(3, CD, CL)
        sent_coords = jnp.einsum("hc,xck->xhk", halo_table, blocks, precision=exact).reshape(
            3, HALO * CL
        )
        from_above = from_behind(sent_coords, "slab", -1) + lift
        extended = jnp.concatenate([blocks, from_above.reshape(3, HALO, CL)], 1)
        forces, energy = slab_pairs(extended, param_all, tile_list, live_count)
        returned = from_behind(forces[:, CD:].reshape(3, HALO * CL), "slab", 1)
        back_home = jnp.einsum(
            "hc,xhk->xck", halo_table, returned.reshape(3, HALO, CL), precision=exact
        )
        local_forces = forces[:, :CD] + back_home
        return (local_forces.reshape(3, atoms_here), energy)

    def verlet_step(step_idx, carry):
        coords, speeds, forces, energy = carry
        speeds = speeds + half_step * forces * inv_mass
        coords = coords + time_step * speeds
        forces, energy = evaluate(coords)
        speeds = speeds + half_step * forces * inv_mass
        return (coords, speeds, forces, energy)

    forces, energy = evaluate(coords)
    coords, speeds, forces, energy = lax.fori_loop(
        0, STEPS, verlet_step, (coords, speeds, forces, energy)
    )
    total_energy = slab_sum(energy)
    potential = (total_energy / (atoms_here * lax.axis_size("slab"))).reshape(1)
    state = jnp.concatenate([coords, speeds], 0)
    swapped = exchange(state, swap_pairs)
    return (swapped[:3][None], swapped[3:][None], potential)


def slab_sum(value):
    count = lax.axis_size("slab")
    stride = 1
    while stride < count:
        pairs = [(source, source ^ stride) for source in range(count)]
        value = value + lax.ppermute(value, "slab", pairs)
        stride *= 2
    return value


def solution(mesh):
    in_specs = (
        P("rep", None, "slab"),
        P("rep", None, "slab"),
        P("slab"),
        P("slab"),
        P("slab"),
        P("rep"),
        P("rep", None, "slab"),
        P("rep", "slab"),
        P("rep", "slab"),
        P(),
    )
    out_specs = (P("rep", None, "slab"), P("rep", None, "slab"), P("rep"))
    return jax.shard_map(local, mesh=mesh, in_specs=in_specs, out_specs=out_specs, check_vma=False)
```
